512 devices in a mesh: seq: 64 (over y, x, core), ch: 8 (over z).
Axes of the slice: x: 4, y: 8, z: 8, core: 2. Of those that a mesh axis runs over, the one named last changes fastest.
Arguments:
- signal: bfloat16 [1536, 32768], P('ch', 'seq'), may hold values from -16 to 16
- input_norm_gain: float32 [1536], P('ch'), may hold values from 0.25 to 1.75
- value_weight: bfloat16 [1536, 1536], P('seq', 'ch'), may hold values from -0.15625 to 0.15625
- gate_weight: bfloat16 [1536, 1536], P('seq', 'ch'), may hold values from -0.15625 to 0.15625
- depth_taps: float32 [31, 1536], P(None, 'ch'), may hold values from -1 to 1
- cotangent: bfloat16 [1536, 32768], P('ch', 'seq'), may hold values from -6 to 6
Outputs:
- output: bfloat16 [1536, 32768], P('ch', 'seq')
- signal_gradient: bfloat16 [1536, 32768], P('ch', 'seq')
- grad_value: float32 [1536, 1536], P('seq', 'ch')
- grad_gate: float32 [1536, 1536], P('seq', 'ch')
- grad_taps: float32 [31, 1536], P(None, 'ch')
- gain_gradient: float32 [1536], P('ch')
The draws below stay inside these ranges and needn't reach their ends.
All inputs are finite; a program needn't handle non-finite values.
Results may differ from the reference program's by a relative error of at most 0.02.
Values may be sent and summed in bfloat16 or wider, within the bound.
No kernel may reach another device: no remote copies, remote signals or barrier semaphores. Data moves between devices by JAX's collectives and lax.ppermute only.
A program may use at most 64 MiB of HBM per device.

```python
import jax
import jax.numpy as jnp
from jax import lax

D = 1536
KTAPS = 31
FRAMES = 32768
N_CH = 8


def with_spikes(drawn, own_key, source, target, parts, factor):
    owner, partner = [(jnp.arange(drawn.shape[dim]) // (drawn.shape[dim] // parts)).reshape([-1 if axis == dim else 1 for axis in range(drawn.ndim)]) for dim in (source, target)]
    chosen = jax.random.permutation(own_key, parts)[partner]
    strong = (owner == chosen) | (owner == (partner + parts // 2) % parts)
    return jnp.where(strong, factor * drawn, drawn)


def level_of(stream_key, dims, cuts, low, largest):
    gain = 1.0
    for dim, shards_of in cuts:
        draws = jax.random.uniform(jax.random.fold_in(jax.random.fold_in(stream_key, 6), dim), (shards_of,), jnp.float32, low / len(cuts), largest / len(cuts))
        gain = gain * jnp.repeat(jnp.exp(draws), dims[dim] // shards_of).reshape((-1,) + (1,) * (len(dims) - 1 - dim))
    return gain


def scatter_about(stream_key, extent, width, most, cuts=(), held_as=jnp.bfloat16):
    drawn = jax.random.normal(stream_key, extent, jnp.float32) * width
    if len(cuts) > 0:
        drawn = level_of(stream_key, extent, cuts, -0.22, 0.18) * drawn
    return jnp.clip(drawn, min=-most, max=most).astype(held_as)


def gaussian_with(own_key, shape, deviation, most, pieces, heavy, kind=jnp.bfloat16):
    values = deviation * jax.random.normal(own_key, shape, jnp.float32)
    if pieces:
        values = values * level_of(own_key, shape, pieces, -0.22, 0.18)
    return jnp.clip(with_spikes(values, jax.random.fold_in(own_key, 3), *heavy), -most, most).astype(kind)


def setup_inputs(seed: int = 0) -> dict:
    seeds = jax.random.split(jax.random.key(seed), 7)
    signal = gaussian_with(seeds[0], (D, FRAMES), 1.0, 16.0, ((0, 8), (1, 64)), (1, 0, 64, 4.0))
    input_norm_gain = jnp.clip(1.0 + 0.15 * jax.random.normal(seeds[1], (D,), jnp.float32), 0.25, 1.75)
    value_weight = scatter_about(seeds[2], (D, D), D ** -0.5, 0.15625, ((0, 64), (1, 8)))
    gate_weight = scatter_about(seeds[3], (D, D), D ** -0.5, 0.15625, ((0, 64), (1, 8)))
    depth_taps = scatter_about(seeds[4], (KTAPS, D), KTAPS ** -0.5, 1.0, ((1, 8),), jnp.float32)
    cotangent = scatter_about(seeds[5], (D, FRAMES), 1.0, 6.0, ((0, 8), (1, 64)))
    return dict(signal=signal, input_norm_gain=input_norm_gain, value_weight=value_weight, gate_weight=gate_weight, depth_taps=depth_taps, cotangent=cotangent)


def standardize_rows(rows_in):
    values = rows_in.astype(jnp.float32)
    average = lax.optimization_barrier(jnp.mean(values, -1, keepdims=True))
    centred = values - average
    spread = lax.optimization_barrier(jnp.mean(centred * centred, -1, keepdims=True))
    inverse_deviation = lax.rsqrt(spread + 1e-05)
    return (centred * inverse_deviation, inverse_deviation)

def product(left, right):
    return jnp.dot(left.astype(jnp.float32), right.astype(jnp.float32), preferred_element_type=jnp.float32)

def reference(signal, input_norm_gain, value_weight, gate_weight, depth_taps, cotangent):
    reach = KTAPS // 2
    frame_leading_layout = signal.T
    cot_major = cotangent.T
    centered_unit, inverse_deviation = standardize_rows(frame_leading_layout)
    normalized_signal = (centered_unit * input_norm_gain).astype(jnp.bfloat16)
    value = product(normalized_signal, value_weight)
    gate = product(normalized_signal, gate_weight)
    sig_gate = jax.nn.sigmoid(gate)
    glued = (value * sig_gate).astype(jnp.bfloat16)
    glued_pad = jnp.pad(glued.astype(jnp.float32), ((reach, reach), (0, 0)))
    pre = jnp.zeros((FRAMES, D), jnp.float32)
    for offset in range(KTAPS):
        pre = pre + depth_taps[offset] * glued_pad[offset:offset + FRAMES]
    sig_pre = jax.nn.sigmoid(pre)
    output = (pre * sig_pre).astype(jnp.bfloat16)
    grad_pre = (cot_major.astype(jnp.float32) * sig_pre * (1.0 + pre * (1.0 - sig_pre))).astype(jnp.bfloat16)
    grad_pre_f = grad_pre.astype(jnp.float32)
    grad_pad = jnp.pad(grad_pre_f, ((reach, reach), (0, 0)))
    grad_glued = jnp.zeros((FRAMES, D), jnp.float32)
    tap_rows = []
    for offset in range(KTAPS):
        lead = 2 * reach - offset
        grad_glued = grad_glued + depth_taps[offset] * grad_pad[lead:lead + FRAMES]
        tap_rows.append(lax.optimization_barrier(jnp.sum(glued_pad[offset:offset + FRAMES] * grad_pre_f, 0)))
    grad_taps = jnp.stack(tap_rows, 0)
    grad_v = (grad_glued * sig_gate).astype(jnp.bfloat16)
    grad_g = (grad_glued * value * sig_gate * (1.0 - sig_gate)).astype(jnp.bfloat16)
    normed_major = normalized_signal.T
    grad_value = product(normed_major, grad_v)
    grad_gate = product(normed_major, grad_g)
    group_cols = D // N_CH
    normalized_gradient = jnp.zeros((FRAMES, D), jnp.float32)
    for group in range(N_CH):
        first = group * group_cols
        last = first + group_cols
        partial_sum = product(grad_v[:, first:last], value_weight[:, first:last].T)
        partial_sum = partial_sum + product(grad_g[:, first:last], gate_weight[:, first:last].T)
        rounded = lax.optimization_barrier(partial_sum.astype(jnp.bfloat16))
        normalized_gradient = normalized_gradient + rounded.astype(jnp.float32)
    scaled_signal = normalized_gradient * input_norm_gain
    first_moment = lax.optimization_barrier(jnp.mean(scaled_signal, -1, keepdims=True))
    second_moment = lax.optimization_barrier(jnp.mean(scaled_signal * centered_unit, -1, keepdims=True))
    signal_gradient = (inverse_deviation * (scaled_signal - first_moment - centered_unit * second_moment)).astype(jnp.bfloat16)
    gain_gradient = lax.optimization_barrier(jnp.sum(normalized_gradient * centered_unit, 0))
    return (output.T, signal_gradient.T, grad_value, grad_gate, grad_taps, gain_gradient)
```

```python
import jax
import jax.numpy as jnp
from jax import lax
from jax.sharding import PartitionSpec as P


def extended(cells, sides, width):
    for axis, dim in sides:
        count = lax.axis_size(axis)
        ends = count - 1
        head = lax.slice_in_dim(cells, 0, width, axis=dim)
        tail = lax.slice_in_dim(cells, cells.shape[dim] - width, cells.shape[dim], axis=dim)
        cells = jnp.concatenate(
            [
                lax.ppermute(tail, axis, [(i, (i + 1) % count) for i in range(ends)]),
                cells,
                lax.ppermute(head, axis, [((i + 1) % count, i) for i in range(ends)]),
            ],
            axis=dim,
        )
    return cells


def standardize_rows(columns_in):
    values = columns_in.astype(jnp.float32)
    average = jnp.mean(values, 0, keepdims=True)
    centred = values - average
    spread = jnp.mean(centred * centred, 0, keepdims=True)
    inverse_deviation = lax.rsqrt(spread + 1e-05)
    return (centred * inverse_deviation, inverse_deviation)


def depthwise(padded, kernel):
    channels = padded.shape[0]
    result = lax.conv_general_dilated(
        padded[None],
        kernel,
        (1,),
        "VALID",
        dimension_numbers=("NCH", "OIH", "NCH"),
        feature_group_count=channels,
        precision=lax.Precision.HIGHEST,
    )
    return result[0]


def shards(signal, input_norm_gain, value_weight, gate_weight, depth_taps, cotangent):
    local_cols = signal.shape[0]
    seq_position = lax.axis_index("seq")
    channel_position = lax.axis_index("ch")
    reach = depth_taps.shape[0] // 2
    complete_signal = lax.all_gather(signal, "ch", axis=0, tiled=True)
    complete_gain = lax.all_gather(input_norm_gain, "ch", axis=0, tiled=True)
    centered_unit, inverse_deviation = standardize_rows(complete_signal)
    normalized_signal = (centered_unit * complete_gain[:, None]).astype(jnp.bfloat16)
    centered_unit_rows = lax.dynamic_slice_in_dim(
        centered_unit, channel_position * local_cols, local_cols, 0
    )
    stacked = jnp.concatenate([value_weight, gate_weight], 1)
    gathered = lax.all_gather(stacked, "seq", axis=0, tiled=True)
    mixed = lax.dot_general(
        gathered, normalized_signal, (((0,), (0,)), ((), ())), preferred_element_type=jnp.float32
    )
    value = mixed[:local_cols]
    gate = mixed[local_cols:]
    sig_gate = jax.nn.sigmoid(gate)
    glued = (value * sig_gate).astype(jnp.bfloat16)
    glued_pad = extended(glued, (("seq", 1),), reach).astype(jnp.float32)
    forward_kernel = depth_taps.T[:, None, :]
    pre = depthwise(glued_pad, forward_kernel)
    sig_pre = jax.nn.sigmoid(pre)
    output = (pre * sig_pre).astype(jnp.bfloat16)
    grad_pre = (cotangent.astype(jnp.float32) * sig_pre * (1.0 + pre * (1.0 - sig_pre))).astype(
        jnp.bfloat16
    )
    grad_pre_f = grad_pre.astype(jnp.float32)
    grad_pad = extended(grad_pre, (("seq", 1),), reach).astype(jnp.float32)
    grad_glued = depthwise(grad_pad, forward_kernel[:, :, ::-1])
    tap_partial = depthwise(glued_pad, grad_pre_f[:, None, :]).T
    grad_v = (grad_glued * sig_gate).astype(jnp.bfloat16)
    grad_g = (grad_glued * value * sig_gate * (1.0 - sig_gate)).astype(jnp.bfloat16)
    grad_both = jnp.concatenate([grad_v, grad_g], 0)
    weight_partial = lax.dot_general(
        normalized_signal,
        grad_both,
        (((1,), (1,)), ((), ())),
        preferred_element_type=jnp.float32,
    )
    normed_term = jnp.dot(gathered, grad_both, preferred_element_type=jnp.float32)
    normalized_gradient = lax.psum_scatter(
        normed_term.astype(jnp.bfloat16), "ch", scatter_dimension=0, tiled=True
    ).astype(jnp.float32)
    scaled_signal = normalized_gradient * input_norm_gain[:, None]
    moments = jnp.concatenate(
        [
            jnp.sum(scaled_signal, 0, keepdims=True),
            jnp.sum(scaled_signal * centered_unit_rows, 0, keepdims=True),
        ],
        0,
    )
    moments = lax.psum(moments, "ch") * (1.0 / complete_signal.shape[0])
    inverse_rows = inverse_deviation
    signal_gradient = (
        inverse_rows * (scaled_signal - moments[0:1] - centered_unit_rows * moments[1:2])
    ).astype(jnp.bfloat16)
    gain_portion = jnp.sum(normalized_gradient * centered_unit_rows, 1)
    extra = jnp.concatenate([tap_partial, gain_portion[None]], 0)
    extra = jnp.pad(extra, ((0, 0), (0, weight_partial.shape[1] - extra.shape[1])))
    summed = lax.psum(jnp.concatenate([weight_partial, extra], 0), "seq")
    rows = value_weight.shape[0]
    weight_sums = lax.dynamic_slice_in_dim(summed, seq_position * rows, rows, 0)
    grad_value = weight_sums[:, :local_cols]
    grad_gate = weight_sums[:, local_cols:]
    taps_rows = depth_taps.shape[0]
    full_rows = weight_partial.shape[0]
    grad_taps = summed[full_rows : full_rows + taps_rows, :local_cols]
    gain_gradient = summed[full_rows + taps_rows, :local_cols]
    return (output, signal_gradient, grad_value, grad_gate, grad_taps, gain_gradient)


def solution(mesh):
    placed = (
        P("ch", "seq"),
        P("ch"),
        P("seq", "ch"),
        P("seq", "ch"),
        P(None, "ch"),
        P("ch", "seq"),
    )
    return jax.shard_map(
        shards,
        mesh=mesh,
        in_specs=placed,
        out_specs=(
            P("ch", "seq"),
            P("ch", "seq"),
            P("seq", "ch"),
            P("seq", "ch"),
            P(None, "ch"),
            P("ch"),
        ),
        check_vma=False,
    )
```

```python
import jax
import jax.numpy as jnp
from jax import lax
from jax.sharding import PartitionSpec as P


def extended(cells, sides, width):
    for axis, dim in sides:
        count = lax.axis_size(axis)
        ends = count - 1
        head = lax.slice_in_dim(cells, 0, width, axis=dim)
        tail = lax.slice_in_dim(cells, cells.shape[dim] - width, cells.shape[dim], axis=dim)
        cells = jnp.concatenate(
            [
                lax.ppermute(tail, axis, [(i, (i + 1) % count) for i in range(ends)]),
                cells,
                lax.ppermute(head, axis, [((i + 1) % count, i) for i in range(ends)]),
            ],
            axis=dim,
        )
    return cells


def standardize_rows(columns_in):
    values = columns_in.astype(jnp.float32)
    average = jnp.mean(values, 0, keepdims=True)
    centred = values - average
    spread = jnp.mean(centred * centred, 0, keepdims=True)
    inverse_deviation = lax.rsqrt(spread + 1e-05)
    return (centred * inverse_deviation, inverse_deviation)


def depthwise(padded, kernel):
    channels = padded.shape[0]
    result = lax.conv_general_dilated(
        padded[None],
        kernel,
        (1,),
        "VALID",
        dimension_numbers=("NCH", "OIH", "NCH"),
        feature_group_count=channels,
        precision=lax.Precision.HIGHEST,
    )
    return result[0]


def gather_by_exchange(block, axis):
    count = lax.axis_size(axis)
    copies = jnp.broadcast_to(block[None], (count,) + block.shape)
    return lax.all_to_all(copies, axis, 0, 0, tiled=False)


def bf16_pieces(values, pieces):
    parts = []
    rest = values
    for _ in range(pieces):
        part = rest.astype(jnp.bfloat16)
        parts.append(part)
        rest = rest - part.astype(jnp.float32)
    return parts


def shards(signal, input_norm_gain, value_weight, gate_weight, depth_taps, cotangent):
    local_cols, frames = signal.shape
    groups = lax.axis_size("ch")
    blocks = lax.axis_size("seq")
    channel_position = lax.axis_index("ch")
    reach = depth_taps.shape[0] // 2
    gain_rows = jnp.stack(bf16_pieces(input_norm_gain, 3), 0)
    gain_rows = jnp.pad(gain_rows, ((0, 13), (0, frames - local_cols)))
    arrived = gather_by_exchange(jnp.concatenate([signal, gain_rows], 0), "ch")
    complete_signal = arrived[:, :local_cols].reshape(groups * local_cols, frames)
    gain_parts = arrived[:, local_cols : local_cols + 3, :local_cols].astype(jnp.float32)
    complete_gain = ((gain_parts[:, 0] + gain_parts[:, 1]) + gain_parts[:, 2]).reshape(-1)
    centered_unit, inverse_deviation = standardize_rows(complete_signal)
    normalized_signal = (centered_unit * complete_gain[:, None]).astype(jnp.bfloat16)
    centered_unit_rows = lax.dynamic_slice_in_dim(
        centered_unit, channel_position * local_cols, local_cols, 0
    )
    stacked = jnp.concatenate([value_weight, gate_weight], 1)
    gathered = gather_by_exchange(stacked, "seq").reshape(-1, stacked.shape[1])
    mixed = lax.dot_general(
        gathered, normalized_signal, (((0,), (0,)), ((), ())), preferred_element_type=jnp.float32
    )
    value = mixed[:local_cols]
    gate = mixed[local_cols:]
    sig_gate = jax.nn.sigmoid(gate)
    glued = (value * sig_gate).astype(jnp.bfloat16)
    glued_pad = extended(glued, (("seq", 1),), reach).astype(jnp.float32)
    forward_kernel = depth_taps.T[:, None, :]
    pre = depthwise(glued_pad, forward_kernel)
    sig_pre = jax.nn.sigmoid(pre)
    output = (pre * sig_pre).astype(jnp.bfloat16)
    grad_pre = (cotangent.astype(jnp.float32) * sig_pre * (1.0 + pre * (1.0 - sig_pre))).astype(
        jnp.bfloat16
    )
    grad_pre_f = grad_pre.astype(jnp.float32)
    grad_pad = extended(grad_pre, (("seq", 1),), reach).astype(jnp.float32)
    grad_glued = depthwise(grad_pad, forward_kernel[:, :, ::-1])
    tap_partial = depthwise(glued_pad, grad_pre_f[:, None, :]).T
    grad_v = (grad_glued * sig_gate).astype(jnp.bfloat16)
    grad_g = (grad_glued * value * sig_gate * (1.0 - sig_gate)).astype(jnp.bfloat16)
    grad_both = jnp.concatenate([grad_v, grad_g], 0)
    weight_partial = lax.dot_general(
        normalized_signal,
        grad_both,
        (((1,), (1,)), ((), ())),
        preferred_element_type=jnp.float32,
    )
    normed_term = jnp.dot(gathered, grad_both, preferred_element_type=jnp.float32).astype(
        jnp.bfloat16
    )
    gain_portion = jnp.sum(normed_term.astype(jnp.float32) * centered_unit, 1)
    width = weight_partial.shape[1]
    taps_rows = depth_taps.shape[0]
    extra = jnp.pad(tap_partial, ((0, 1), (0, 0))).reshape(-1, width)
    extra = jnp.concatenate([extra, gain_portion.reshape(-1, width)], 0)
    rows = value_weight.shape[0]
    outgoing = jnp.concatenate(
        [
            weight_partial.reshape(blocks, rows, width),
            jnp.broadcast_to(extra[None], (blocks,) + extra.shape),
        ],
        1,
    )
    summed = jnp.sum(lax.all_to_all(outgoing, "seq", 0, 0, tiled=False), 0)
    grad_value = summed[:rows, :local_cols]
    grad_gate = summed[:rows, local_cols:]
    taps_end = rows + (taps_rows + 1) * local_cols // width
    grad_taps = summed[rows:taps_end].reshape(taps_rows + 1, local_cols)[:taps_rows]
    gain_seq_sum = summed[taps_end:].reshape(-1)
    partials = lax.all_to_all(
        normed_term.reshape(groups, local_cols, frames), "ch", 0, 0, tiled=False
    )
    normalized_gradient = jnp.sum(partials.astype(jnp.float32), 0)
    scaled_signal = normalized_gradient * input_norm_gain[:, None]
    moments = jnp.concatenate(
        [
            jnp.sum(scaled_signal, 0),
            jnp.sum(scaled_signal * centered_unit_rows, 0),
            gain_seq_sum,
        ],
        0,
    )
    moments = lax.psum(moments, "ch")
    first_moment = moments[:frames] * (1.0 / complete_signal.shape[0])
    second_moment = moments[frames : 2 * frames] * (1.0 / complete_signal.shape[0])
    signal_gradient = (
        inverse_deviation
        * (scaled_signal - first_moment[None] - centered_unit_rows * second_moment[None])
    ).astype(jnp.bfloat16)
    gain_gradient = lax.dynamic_slice_in_dim(
        moments[2 * frames :], channel_position * local_cols, local_cols, 0
    )
    return (output, signal_gradient, grad_value, grad_gate, grad_taps, gain_gradient)


def solution(mesh):
    placed = (
        P("ch", "seq"),
        P("ch"),
        P("seq", "ch"),
        P("seq", "ch"),
        P(None, "ch"),
        P("ch", "seq"),
    )
    return jax.shard_map(
        shards,
        mesh=mesh,
        in_specs=placed,
        out_specs=(
            P("ch", "seq"),
            P("ch", "seq"),
            P("seq", "ch"),
            P("seq", "ch"),
            P(None, "ch"),
            P("ch"),
        ),
        check_vma=False,
    )
```

```python
import jax
import jax.numpy as jnp
from jax import lax
from jax.sharding import PartitionSpec as P


def extended(cells, sides, width):
    for axis, dim in sides:
        count = lax.axis_size(axis)
        ends = count - 1
        head = lax.slice_in_dim(cells, 0, width, axis=dim)
        tail = lax.slice_in_dim(cells, cells.shape[dim] - width, cells.shape[dim], axis=dim)
        cells = jnp.concatenate(
            [
                lax.ppermute(tail, axis, [(i, (i + 1) % count) for i in range(ends)]),
                cells,
                lax.ppermute(head, axis, [((i + 1) % count, i) for i in range(ends)]),
            ],
            axis=dim,
        )
    return cells


def standardize_rows(columns_in):
    values = columns_in.astype(jnp.float32)
    average = jnp.mean(values, 0, keepdims=True)
    centred = values - average
    spread = jnp.mean(centred * centred, 0, keepdims=True)
    inverse_deviation = lax.rsqrt(spread + 1e-05)
    return (centred * inverse_deviation, inverse_deviation)


def depthwise(padded, kernel):
    channels = padded.shape[0]
    result = lax.conv_general_dilated(
        padded[None],
        kernel,
        (1,),
        "VALID",
        dimension_numbers=("NCH", "OIH", "NCH"),
        feature_group_count=channels,
        precision=lax.Precision.HIGHEST,
    )
    return result[0]


def gather_by_exchange(block, axis):
    count = lax.axis_size(axis)
    copies = jnp.broadcast_to(block[None], (count,) + block.shape)
    return lax.all_to_all(copies, axis, 0, 0, tiled=False)


def bf16_pieces(values, pieces):
    parts = []
    rest = values
    for _ in range(pieces):
        part = rest.astype(jnp.bfloat16)
        parts.append(part)
        rest = rest - part.astype(jnp.float32)
    return parts


def gather_by_shifts(block, axis):
    count = lax.axis_size(axis)
    position = lax.axis_index(axis)
    pieces = [block]
    for shift in range(1, count):
        pieces.append(
            lax.ppermute(block, axis, [(i, (i - shift) % count) for i in range(count)])
        )
    return jnp.roll(jnp.stack(pieces, 0), position, axis=0)


def reduce_by_shifts(blocks, axis):
    count = lax.axis_size(axis)
    position = lax.axis_index(axis)
    total = lax.dynamic_index_in_dim(blocks, position, 0, keepdims=False).astype(jnp.float32)
    for shift in range(1, count):
        outgoing = lax.dynamic_index_in_dim(blocks, (position + shift) % count, 0, keepdims=False)
        arrived = lax.ppermute(outgoing, axis, [(i, (i + shift) % count) for i in range(count)])
        total = total + arrived.astype(jnp.float32)
    return total


def shards(signal, input_norm_gain, value_weight, gate_weight, depth_taps, cotangent):
    local_cols, frames = signal.shape
    groups = lax.axis_size("ch")
    blocks = lax.axis_size("seq")
    channel_position = lax.axis_index("ch")
    reach = depth_taps.shape[0] // 2
    gain_rows = jnp.stack(bf16_pieces(input_norm_gain, 3), 0)
    gain_rows = jnp.pad(gain_rows, ((0, 13), (0, frames - local_cols)))
    arrived = gather_by_shifts(jnp.concatenate([signal, gain_rows], 0), "ch")
    complete_signal = arrived[:, :local_cols].reshape(groups * local_cols, frames)
    gain_parts = arrived[:, local_cols : local_cols + 3, :local_cols].astype(jnp.float32)
    complete_gain = ((gain_parts[:, 0] + gain_parts[:, 1]) + gain_parts[:, 2]).reshape(-1)
    centered_unit, inverse_deviation = standardize_rows(complete_signal)
    normalized_signal = (centered_unit * complete_gain[:, None]).astype(jnp.bfloat16)
    centered_unit_rows = lax.dynamic_slice_in_dim(
        centered_unit, channel_position * local_cols, local_cols, 0
    )
    stacked = jnp.concatenate([value_weight, gate_weight], 1)
    gathered = gather_by_exchange(stacked, "seq").reshape(-1, stacked.shape[1])
    mixed = lax.dot_general(
        gathered, normalized_signal, (((0,), (0,)), ((), ())), preferred_element_type=jnp.float32
    )
    value = mixed[:local_cols]
    gate = mixed[local_cols:]
    sig_gate = jax.nn.sigmoid(gate)
    glued = (value * sig_gate).astype(jnp.bfloat16)
    glued_pad = extended(glued, (("seq", 1),), reach).astype(jnp.float32)
    forward_kernel = depth_taps.T[:, None, :]
    pre = depthwise(glued_pad, forward_kernel)
    sig_pre = jax.nn.sigmoid(pre)
    output = (pre * sig_pre).astype(jnp.bfloat16)
    grad_pre = (cotangent.astype(jnp.float32) * sig_pre * (1.0 + pre * (1.0 - sig_pre))).astype(
        jnp.bfloat16
    )
    grad_pre_f = grad_pre.astype(jnp.float32)
    grad_pad = extended(grad_pre, (("seq", 1),), reach).astype(jnp.float32)
    grad_glued = depthwise(grad_pad, forward_kernel[:, :, ::-1])
    tap_partial = depthwise(glued_pad, grad_pre_f[:, None, :]).T
    grad_v = (grad_glued * sig_gate).astype(jnp.bfloat16)
    grad_g = (grad_glued * value * sig_gate * (1.0 - sig_gate)).astype(jnp.bfloat16)
    grad_both = jnp.concatenate([grad_v, grad_g], 0)
    weight_partial = lax.dot_general(
        normalized_signal,
        grad_both,
        (((1,), (1,)), ((), ())),
        preferred_element_type=jnp.float32,
    )
    normed_term = jnp.dot(gathered, grad_both, preferred_element_type=jnp.float32).astype(
        jnp.bfloat16
    )
    gain_portion = jnp.sum(normed_term.astype(jnp.float32) * centered_unit, 1)
    width = weight_partial.shape[1]
    taps_rows = depth_taps.shape[0]
    extra = jnp.pad(tap_partial, ((0, 1), (0, 0))).reshape(-1, width)
    extra = jnp.concatenate([extra, gain_portion.reshape(-1, width)], 0)
    rows = value_weight.shape[0]
    outgoing = jnp.concatenate(
        [
            weight_partial.reshape(blocks, rows, width),
            jnp.broadcast_to(extra[None], (blocks,) + extra.shape),
        ],
        1,
    )
    summed = jnp.sum(lax.all_to_all(outgoing, "seq", 0, 0, tiled=False), 0)
    grad_value = summed[:rows, :local_cols]
    grad_gate = summed[:rows, local_cols:]
    taps_end = rows + (taps_rows + 1) * local_cols // width
    grad_taps = summed[rows:taps_end].reshape(taps_rows + 1, local_cols)[:taps_rows]
    gain_seq_sum = summed[taps_end:].reshape(-1)
    normalized_gradient = reduce_by_shifts(
        normed_term.reshape(groups, local_cols, frames), "ch"
    )
    scaled_signal = normalized_gradient * input_norm_gain[:, None]
    moments = jnp.concatenate(
        [
            jnp.sum(scaled_signal, 0),
            jnp.sum(scaled_signal * centered_unit_rows, 0),
            gain_seq_sum,
        ],
        0,
    )
    moments = lax.psum(moments, "ch")
    first_moment = moments[:frames] * (1.0 / complete_signal.shape[0])
    second_moment = moments[frames : 2 * frames] * (1.0 / complete_signal.shape[0])
    signal_gradient = (
        inverse_deviation
        * (scaled_signal - first_moment[None] - centered_unit_rows * second_moment[None])
    ).astype(jnp.bfloat16)
    gain_gradient = lax.dynamic_slice_in_dim(
        moments[2 * frames :], channel_position * local_cols, local_cols, 0
    )
    return (output, signal_gradient, grad_value, grad_gate, grad_taps, gain_gradient)


def solution(mesh):
    placed = (
        P("ch", "seq"),
        P("ch"),
        P("seq", "ch"),
        P("seq", "ch"),
        P(None, "ch"),
        P("ch", "seq"),
    )
    return jax.shard_map(
        shards,
        mesh=mesh,
        in_specs=placed,
        out_specs=(
            P("ch", "seq"),
            P("ch", "seq"),
            P("seq", "ch"),
            P("seq", "ch"),
            P(None, "ch"),
            P("ch"),
        ),
        check_vma=False,
    )
```

```python
import jax
import jax.numpy as jnp
from jax import lax
from jax.sharding import PartitionSpec as P


def extended(cells, sides, width):
    for axis, dim in sides:
        count = lax.axis_size(axis)
        ends = count - 1
        head = lax.slice_in_dim(cells, 0, width, axis=dim)
        tail = lax.slice_in_dim(cells, cells.shape[dim] - width, cells.shape[dim], axis=dim)
        cells = jnp.concatenate(
            [
                lax.ppermute(tail, axis, [(i, (i + 1) % count) for i in range(ends)]),
                cells,
                lax.ppermute(head, axis, [((i + 1) % count, i) for i in range(ends)]),
            ],
            axis=dim,
        )
    return cells


def standardize_rows(columns_in):
    values = columns_in.astype(jnp.float32)
    average = jnp.mean(values, 0, keepdims=True)
    centred = values - average
    spread = jnp.mean(centred * centred, 0, keepdims=True)
    inverse_deviation = lax.rsqrt(spread + 1e-05)
    return (centred * inverse_deviation, inverse_deviation)


def depthwise(padded, kernel):
    channels = padded.shape[0]
    result = lax.conv_general_dilated(
        padded[None],
        kernel,
        (1,),
        "VALID",
        dimension_numbers=("NCH", "OIH", "NCH"),
        feature_group_count=channels,
        precision=lax.Precision.HIGHEST,
    )
    return result[0]


def gather_by_exchange(block, axis):
    count = lax.axis_size(axis)
    copies = jnp.broadcast_to(block[None], (count,) + block.shape)
    return lax.all_to_all(copies, axis, 0, 0, tiled=False)


def bf16_pieces(values, pieces):
    parts = []
    rest = values
    for _ in range(pieces):
        part = rest.astype(jnp.bfloat16)
        parts.append(part)
        rest = rest - part.astype(jnp.float32)
    return parts


def gather_by_shifts(block, axis):
    count = lax.axis_size(axis)
    position = lax.axis_index(axis)
    pieces = [block]
    for shift in range(1, count):
        pieces.append(
            lax.ppermute(block, axis, [(i, (i - shift) % count) for i in range(count)])
        )
    return jnp.roll(jnp.stack(pieces, 0), position, axis=0)


def reduce_by_shifts(blocks, axis):
    count = lax.axis_size(axis)
    position = lax.axis_index(axis)
    total = lax.dynamic_index_in_dim(blocks, position, 0, keepdims=False).astype(jnp.float32)
    for shift in range(1, count):
        outgoing = lax.dynamic_index_in_dim(blocks, (position + shift) % count, 0, keepdims=False)
        arrived = lax.ppermute(outgoing, axis, [(i, (i + shift) % count) for i in range(count)])
        total = total + arrived.astype(jnp.float32)
    return total


def shards(signal, input_norm_gain, value_weight, gate_weight, depth_taps, cotangent):
    local_cols, frames = signal.shape
    groups = lax.axis_size("ch")
    blocks = lax.axis_size("seq")
    channel_position = lax.axis_index("ch")
    reach = depth_taps.shape[0] // 2
    gain_rows = jnp.stack(bf16_pieces(input_norm_gain, 3), 0)
    gain_rows = jnp.pad(gain_rows, ((0, 13), (0, frames - local_cols)))
    arrived = gather_by_shifts(jnp.concatenate([signal, gain_rows], 0), "ch")
    complete_signal = arrived[:, :local_cols].reshape(groups * local_cols, frames)
    gain_parts = arrived[:, local_cols : local_cols + 3, :local_cols].astype(jnp.float32)
    complete_gain = ((gain_parts[:, 0] + gain_parts[:, 1]) + gain_parts[:, 2]).reshape(-1)
    centered_unit, inverse_deviation = standardize_rows(complete_signal)
    normalized_signal = (centered_unit * complete_gain[:, None]).astype(jnp.bfloat16)
    centered_unit_rows = lax.dynamic_slice_in_dim(
        centered_unit, channel_position * local_cols, local_cols, 0
    )
    stacked = jnp.concatenate([value_weight, gate_weight], 1)
    gathered = gather_by_exchange(stacked, "seq").reshape(-1, stacked.shape[1])
    mixed = lax.dot_general(
        gathered, normalized_signal, (((0,), (0,)), ((), ())), preferred_element_type=jnp.float32
    )
    value = mixed[:local_cols]
    gate = mixed[local_cols:]
    sig_gate = jax.nn.sigmoid(gate)
    glued = (value * sig_gate).astype(jnp.bfloat16)
    glued_pad = extended(glued, (("seq", 1),), reach).astype(jnp.float32)
    forward_kernel = depth_taps.T[:, None, :]
    pre = depthwise(glued_pad, forward_kernel)
    sig_pre = jax.nn.sigmoid(pre)
    output = (pre * sig_pre).astype(jnp.bfloat16)
    grad_pre = (cotangent.astype(jnp.float32) * sig_pre * (1.0 + pre * (1.0 - sig_pre))).astype(
        jnp.bfloat16
    )
    grad_pre_f = grad_pre.astype(jnp.float32)
    grad_pad = extended(grad_pre, (("seq", 1),), reach).astype(jnp.float32)
    grad_glued = depthwise(grad_pad, forward_kernel[:, :, ::-1])
    tap_partial = depthwise(glued_pad, grad_pre_f[:, None, :]).T
    grad_v = (grad_glued * sig_gate).astype(jnp.bfloat16)
    grad_g = (grad_glued * value * sig_gate * (1.0 - sig_gate)).astype(jnp.bfloat16)
    grad_both = jnp.concatenate([grad_v, grad_g], 0)
    weight_partial = lax.dot_general(
        normalized_signal,
        grad_both,
        (((1,), (1,)), ((), ())),
        preferred_element_type=jnp.float32,
    )
    normed_term = jnp.dot(gathered, grad_both, preferred_element_type=jnp.float32).astype(
        jnp.bfloat16
    )
    width = weight_partial.shape[1]
    rows = value_weight.shape[0]
    taps_rows = depth_taps.shape[0]
    taps_flat = jnp.pad(tap_partial, ((0, 1), (0, 0))).reshape(blocks, -1)
    piece = taps_flat.shape[1]
    outgoing = jnp.concatenate([weight_partial.reshape(blocks, rows * width), taps_flat], 1)
    summed = jnp.sum(lax.all_to_all(outgoing, "seq", 0, 0, tiled=False), 0)
    weight_sums = summed[: rows * width].reshape(rows, width)
    grad_value = weight_sums[:, :local_cols]
    grad_gate = weight_sums[:, local_cols:]
    normalized_gradient = reduce_by_shifts(
        normed_term.reshape(groups, local_cols, frames), "ch"
    )
    scaled_signal = normalized_gradient * input_norm_gain[:, None]
    moments = jnp.stack(
        [
            jnp.sum(scaled_signal, 0),
            jnp.sum(scaled_signal * centered_unit_rows, 0),
        ],
        0,
    )
    moments = lax.psum(moments, "ch") * (1.0 / complete_signal.shape[0])
    signal_gradient = (
        inverse_deviation
        * (scaled_signal - moments[0:1] - centered_unit_rows * moments[1:2])
    ).astype(jnp.bfloat16)
    gain_portion = jnp.sum(normalized_gradient * centered_unit_rows, 1)
    last = jnp.concatenate([summed[rows * width :], gain_portion], 0)
    finished = gather_by_exchange(last, "seq")
    grad_taps = finished[:, :piece].reshape(-1)[: taps_rows * local_cols].reshape(
        taps_rows, local_cols
    )
    gain_gradient = jnp.sum(finished[:, piece:], 0)
    return (output, signal_gradient, grad_value, grad_gate, grad_taps, gain_gradient)


def solution(mesh):
    placed = (
        P("ch", "seq"),
        P("ch"),
        P("seq", "ch"),
        P("seq", "ch"),
        P(None, "ch"),
        P("ch", "seq"),
    )
    return jax.shard_map(
        shards,
        mesh=mesh,
        in_specs=placed,
        out_specs=(
            P("ch", "seq"),
            P("ch", "seq"),
            P("seq", "ch"),
            P("seq", "ch"),
            P(None, "ch"),
            P("ch"),
        ),
        check_vma=False,
    )
```

```python
import jax
import jax.numpy as jnp
from jax import lax
from jax.sharding import PartitionSpec as P


def extended(cells, sides, width):
    for axis, dim in sides:
        count = lax.axis_size(axis)
        ends = count - 1
        head = lax.slice_in_dim(cells, 0, width, axis=dim)
        tail = lax.slice_in_dim(cells, cells.shape[dim] - width, cells.shape[dim], axis=dim)
        cells = jnp.concatenate(
            [
                lax.ppermute(tail, axis, [(i, (i + 1) % count) for i in range(ends)]),
                cells,
                lax.ppermute(head, axis, [((i + 1) % count, i) for i in range(ends)]),
            ],
            axis=dim,
        )
    return cells


def standardize_rows(columns_in):
    values = columns_in.astype(jnp.float32)
    average = jnp.mean(values, 0, keepdims=True)
    centred = values - average
    spread = jnp.mean(centred * centred, 0, keepdims=True)
    inverse_deviation = lax.rsqrt(spread + 1e-05)
    return (centred * inverse_deviation, inverse_deviation)


def depthwise(padded, kernel):
    channels = padded.shape[0]
    result = lax.conv_general_dilated(
        padded[None],
        kernel,
        (1,),
        "VALID",
        dimension_numbers=("NCH", "OIH", "NCH"),
        feature_group_count=channels,
        precision=lax.Precision.HIGHEST,
    )
    return result[0]


def gather_by_exchange(block, axis):
    count = lax.axis_size(axis)
    copies = jnp.broadcast_to(block[None], (count,) + block.shape)
    return lax.all_to_all(copies, axis, 0, 0, tiled=False)


def bf16_pieces(values, pieces):
    parts = []
    rest = values
    for _ in range(pieces):
        part = rest.astype(jnp.bfloat16)
        parts.append(part)
        rest = rest - part.astype(jnp.float32)
    return parts


def gather_by_shifts(block, axis):
    count = lax.axis_size(axis)
    position = lax.axis_index(axis)
    pieces = [block]
    for shift in range(1, count):
        pieces.append(
            lax.ppermute(block, axis, [(i, (i - shift) % count) for i in range(count)])
        )
    return jnp.roll(jnp.stack(pieces, 0), position, axis=0)


def reduce_by_shifts(blocks, axis):
    count = lax.axis_size(axis)
    position = lax.axis_index(axis)
    total = lax.dynamic_index_in_dim(blocks, position, 0, keepdims=False).astype(jnp.float32)
    for shift in range(1, count):
        outgoing = lax.dynamic_index_in_dim(blocks, (position + shift) % count, 0, keepdims=False)
        arrived = lax.ppermute(outgoing, axis, [(i, (i + shift) % count) for i in range(count)])
        total = total + arrived.astype(jnp.float32)
    return total


def shifted_sum(padded, taps, span):
    total = taps[0][:, None] * padded[:, 0:span]
    for k in range(1, taps.shape[0]):
        total = total + taps[k][:, None] * padded[:, k : k + span]
    return total


def shards(signal, input_norm_gain, value_weight, gate_weight, depth_taps, cotangent):
    local_cols, frames = signal.shape
    groups = lax.axis_size("ch")
    blocks = lax.axis_size("seq")
    channel_position = lax.axis_index("ch")
    reach = depth_taps.shape[0] // 2
    gain_rows = jnp.stack(bf16_pieces(input_norm_gain, 3), 0)
    gain_rows = jnp.pad(gain_rows, ((0, 13), (0, frames - local_cols)))
    arrived = gather_by_shifts(jnp.concatenate([signal, gain_rows], 0), "ch")
    complete_signal = arrived[:, :local_cols].reshape(groups * local_cols, frames)
    gain_parts = arrived[:, local_cols : local_cols + 3, :local_cols].astype(jnp.float32)
    complete_gain = ((gain_parts[:, 0] + gain_parts[:, 1]) + gain_parts[:, 2]).reshape(-1)
    centered_unit, inverse_deviation = standardize_rows(complete_signal)
    normalized_signal = (centered_unit * complete_gain[:, None]).astype(jnp.bfloat16)
    centered_unit_rows = lax.dynamic_slice_in_dim(
        centered_unit, channel_position * local_cols, local_cols, 0
    )
    stacked = jnp.concatenate([value_weight, gate_weight], 1)
    gathered = gather_by_exchange(stacked, "seq").reshape(-1, stacked.shape[1])
    mixed = lax.dot_general(
        gathered, normalized_signal, (((0,), (0,)), ((), ())), preferred_element_type=jnp.float32
    )
    value = mixed[:local_cols]
    gate = mixed[local_cols:]
    sig_gate = jax.nn.sigmoid(gate)
    glued = (value * sig_gate).astype(jnp.bfloat16)
    glued_pad = extended(glued, (("seq", 1),), reach).astype(jnp.float32)
    span = glued.shape[1]
    taps_count = depth_taps.shape[0]
    pre = shifted_sum(glued_pad, depth_taps, span)
    sig_pre = jax.nn.sigmoid(pre)
    output = (pre * sig_pre).astype(jnp.bfloat16)
    grad_pre = (cotangent.astype(jnp.float32) * sig_pre * (1.0 + pre * (1.0 - sig_pre))).astype(
        jnp.bfloat16
    )
    grad_pre_f = grad_pre.astype(jnp.float32)
    grad_pad = extended(grad_pre, (("seq", 1),), reach).astype(jnp.float32)
    grad_glued = shifted_sum(grad_pad, depth_taps[::-1], span)
    tap_partial = jnp.stack(
        [jnp.sum(glued_pad[:, k : k + span] * grad_pre_f, 1) for k in range(taps_count)], 0
    )
    grad_v = (grad_glued * sig_gate).astype(jnp.bfloat16)
    grad_g = (grad_glued * value * sig_gate * (1.0 - sig_gate)).astype(jnp.bfloat16)
    grad_both = jnp.concatenate([grad_v, grad_g], 0)
    weight_partial = lax.dot_general(
        normalized_signal,
        grad_both,
        (((1,), (1,)), ((), ())),
        preferred_element_type=jnp.float32,
    )
    normed_term = jnp.dot(gathered, grad_both, preferred_element_type=jnp.float32).astype(
        jnp.bfloat16
    )
    width = weight_partial.shape[1]
    rows = value_weight.shape[0]
    taps_rows = depth_taps.shape[0]
    taps_flat = jnp.pad(tap_partial, ((0, 1), (0, 0))).reshape(blocks, -1)
    piece = taps_flat.shape[1]
    outgoing = jnp.concatenate([weight_partial.reshape(blocks, rows * width), taps_flat], 1)
    summed = jnp.sum(lax.all_to_all(outgoing, "seq", 0, 0, tiled=False), 0)
    weight_sums = summed[: rows * width].reshape(rows, width)
    grad_value = weight_sums[:, :local_cols]
    grad_gate = weight_sums[:, local_cols:]
    normalized_gradient = reduce_by_shifts(
        normed_term.reshape(groups, local_cols, frames), "ch"
    )
    scaled_signal = normalized_gradient * input_norm_gain[:, None]
    moments = jnp.stack(
        [
            jnp.sum(scaled_signal, 0),
            jnp.sum(scaled_signal * centered_unit_rows, 0),
        ],
        0,
    )
    moments = lax.psum(moments, "ch") * (1.0 / complete_signal.shape[0])
    signal_gradient = (
        inverse_deviation
        * (scaled_signal - moments[0:1] - centered_unit_rows * moments[1:2])
    ).astype(jnp.bfloat16)
    gain_portion = jnp.sum(normalized_gradient * centered_unit_rows, 1)
    last = jnp.concatenate([summed[rows * width :], gain_portion], 0)
    finished = gather_by_exchange(last, "seq")
    grad_taps = finished[:, :piece].reshape(-1)[: taps_rows * local_cols].reshape(
        taps_rows, local_cols
    )
    gain_gradient = jnp.sum(finished[:, piece:], 0)
    return (output, signal_gradient, grad_value, grad_gate, grad_taps, gain_gradient)


def solution(mesh):
    placed = (
        P("ch", "seq"),
        P("ch"),
        P("seq", "ch"),
        P("seq", "ch"),
        P(None, "ch"),
        P("ch", "seq"),
    )
    return jax.shard_map(
        shards,
        mesh=mesh,
        in_specs=placed,
        out_specs=(
            P("ch", "seq"),
            P("ch", "seq"),
            P("seq", "ch"),
            P("seq", "ch"),
            P(None, "ch"),
            P("ch"),
        ),
        check_vma=False,
    )
```

```python
import jax
import jax.numpy as jnp
from jax import lax
from jax.sharding import PartitionSpec as P


def extended(cells, sides, width):
    for axis, dim in sides:
        count = lax.axis_size(axis)
        ends = count - 1
        head = lax.slice_in_dim(cells, 0, width, axis=dim)
        tail = lax.slice_in_dim(cells, cells.shape[dim] - width, cells.shape[dim], axis=dim)
        cells = jnp.concatenate(
            [
                lax.ppermute(tail, axis, [(i, (i + 1) % count) for i in range(ends)]),
                cells,
                lax.ppermute(head, axis, [((i + 1) % count, i) for i in range(ends)]),
            ],
            axis=dim,
        )
    return cells


def standardize_rows(columns_in):
    values = columns_in.astype(jnp.float32)
    average = jnp.mean(values, 0, keepdims=True)
    centred = values - average
    spread = jnp.mean(centred * centred, 0, keepdims=True)
    inverse_deviation = lax.rsqrt(spread + 1e-05)
    return (centred * inverse_deviation, inverse_deviation)


def depthwise(padded, kernel):
    channels = padded.shape[0]
    result = lax.conv_general_dilated(
        padded[None],
        kernel,
        (1,),
        "VALID",
        dimension_numbers=("NCH", "OIH", "NCH"),
        feature_group_count=channels,
        precision=lax.Precision.HIGHEST,
    )
    return result[0]


def gather_by_exchange(block, axis):
    count = lax.axis_size(axis)
    copies = jnp.broadcast_to(block[None], (count,) + block.shape)
    return lax.all_to_all(copies, axis, 0, 0, tiled=False)


def bf16_pieces(values, pieces):
    parts = []
    rest = values
    for _ in range(pieces):
        part = rest.astype(jnp.bfloat16)
        parts.append(part)
        rest = rest - part.astype(jnp.float32)
    return parts


def gather_by_shifts(block, axis):
    count = lax.axis_size(axis)
    position = lax.axis_index(axis)
    pieces = [block]
    for shift in range(1, count):
        pieces.append(
            lax.ppermute(block, axis, [(i, (i - shift) % count) for i in range(count)])
        )
    return jnp.roll(jnp.stack(pieces, 0), position, axis=0)


def reduce_by_shifts(blocks, rider, axis):
    count = lax.axis_size(axis)
    position = lax.axis_index(axis)
    total = lax.dynamic_index_in_dim(blocks, position, 0, keepdims=False).astype(jnp.float32)
    riders = rider.astype(jnp.float32)
    rows = blocks.shape[1]
    for shift in range(1, count):
        outgoing = lax.dynamic_index_in_dim(blocks, (position + shift) % count, 0, keepdims=False)
        outgoing = jnp.concatenate([outgoing, rider], 0)
        arrived = lax.ppermute(outgoing, axis, [(i, (i + shift) % count) for i in range(count)])
        total = total + arrived[:rows].astype(jnp.float32)
        riders = riders + arrived[rows:].astype(jnp.float32)
    return total, riders


def shifted_sum(padded, taps, span):
    total = taps[0][:, None] * padded[:, 0:span]
    for k in range(1, taps.shape[0]):
        total = total + taps[k][:, None] * padded[:, k : k + span]
    return total


def shards(signal, input_norm_gain, value_weight, gate_weight, depth_taps, cotangent):
    local_cols, frames = signal.shape
    groups = lax.axis_size("ch")
    blocks = lax.axis_size("seq")
    channel_position = lax.axis_index("ch")
    reach = depth_taps.shape[0] // 2
    gain_rows = jnp.stack(bf16_pieces(input_norm_gain, 3), 0)
    gain_rows = jnp.pad(gain_rows, ((0, 13), (0, frames - local_cols)))
    arrived = lax.all_gather(jnp.concatenate([signal, gain_rows], 0), "ch", axis=0)
    complete_signal = arrived[:, :local_cols].reshape(groups * local_cols, frames)
    gain_parts = arrived[:, local_cols : local_cols + 3, :local_cols].astype(jnp.float32)
    complete_gain = ((gain_parts[:, 0] + gain_parts[:, 1]) + gain_parts[:, 2]).reshape(-1)
    centered_unit, inverse_deviation = standardize_rows(complete_signal)
    normalized_signal = (centered_unit * complete_gain[:, None]).astype(jnp.bfloat16)
    centered_unit_rows = lax.dynamic_slice_in_dim(
        centered_unit, channel_position * local_cols, local_cols, 0
    )
    stacked = jnp.concatenate([value_weight, gate_weight], 1)
    gathered = gather_by_exchange(stacked, "seq").reshape(-1, stacked.shape[1])
    mixed = lax.dot_general(
        gathered, normalized_signal, (((0,), (0,)), ((), ())), preferred_element_type=jnp.float32
    )
    value = mixed[:local_cols]
    gate = mixed[local_cols:]
    sig_gate = jax.nn.sigmoid(gate)
    glued = (value * sig_gate).astype(jnp.bfloat16)
    glued_pad = extended(glued, (("seq", 1),), reach).astype(jnp.float32)
    span = glued.shape[1]
    taps_count = depth_taps.shape[0]
    pre = shifted_sum(glued_pad, depth_taps, span)
    sig_pre = jax.nn.sigmoid(pre)
    output = (pre * sig_pre).astype(jnp.bfloat16)
    grad_pre = (cotangent.astype(jnp.float32) * sig_pre * (1.0 + pre * (1.0 - sig_pre))).astype(
        jnp.bfloat16
    )
    grad_pre_f = grad_pre.astype(jnp.float32)
    grad_pad = extended(grad_pre, (("seq", 1),), reach).astype(jnp.float32)
    grad_glued = shifted_sum(grad_pad, depth_taps[::-1], span)
    tap_partial = jnp.stack(
        [jnp.sum(glued_pad[:, k : k + span] * grad_pre_f, 1) for k in range(taps_count)], 0
    )
    grad_v = (grad_glued * sig_gate).astype(jnp.bfloat16)
    grad_g = (grad_glued * value * sig_gate * (1.0 - sig_gate)).astype(jnp.bfloat16)
    grad_both = jnp.concatenate([grad_v, grad_g], 0)
    weight_partial = lax.dot_general(
        normalized_signal,
        grad_both,
        (((1,), (1,)), ((), ())),
        preferred_element_type=jnp.float32,
    )
    normed_term = jnp.dot(gathered, grad_both, preferred_element_type=jnp.float32).astype(
        jnp.bfloat16
    )
    width = weight_partial.shape[1]
    rows = value_weight.shape[0]
    taps_rows = depth_taps.shape[0]
    taps_flat = jnp.pad(tap_partial, ((0, 1), (0, 0))).reshape(blocks, -1)
    piece = taps_flat.shape[1]
    outgoing = jnp.concatenate([weight_partial.reshape(blocks, rows * width), taps_flat], 1)
    summed = jnp.sum(lax.all_to_all(outgoing, "seq", 0, 0, tiled=False), 0)
    weight_sums = summed[: rows * width].reshape(rows, width)
    grad_value = weight_sums[:, :local_cols]
    grad_gate = weight_sums[:, local_cols:]
    normed_f = normed_term.astype(jnp.float32)
    weighted = normed_f * complete_gain[:, None]
    own_moments = jnp.stack([jnp.sum(weighted, 0), jnp.sum(weighted * centered_unit, 0)], 0)
    moment_rows = jnp.concatenate(bf16_pieces(own_moments, 3), 0)
    moment_rows = jnp.pad(moment_rows, ((0, 16 - moment_rows.shape[0]), (0, 0)))
    normalized_gradient, moment_total = reduce_by_shifts(
        normed_term.reshape(groups, local_cols, frames), moment_rows, "ch"
    )
    scaled_signal = normalized_gradient * input_norm_gain[:, None]
    moments = ((moment_total[0:2] + moment_total[2:4]) + moment_total[4:6]) * (
        1.0 / complete_signal.shape[0]
    )
    signal_gradient = (
        inverse_deviation
        * (scaled_signal - moments[0:1] - centered_unit_rows * moments[1:2])
    ).astype(jnp.bfloat16)
    gain_portion = jnp.sum(normalized_gradient * centered_unit_rows, 1)
    last = jnp.concatenate([summed[rows * width :], gain_portion], 0)
    finished = gather_by_exchange(last, "seq")
    grad_taps = finished[:, :piece].reshape(-1)[: taps_rows * local_cols].reshape(
        taps_rows, local_cols
    )
    gain_gradient = jnp.sum(finished[:, piece:], 0)
    return (output, signal_gradient, grad_value, grad_gate, grad_taps, gain_gradient)


def solution(mesh):
    placed = (
        P("ch", "seq"),
        P("ch"),
        P("seq", "ch"),
        P("seq", "ch"),
        P(None, "ch"),
        P("ch", "seq"),
    )
    return jax.shard_map(
        shards,
        mesh=mesh,
        in_specs=placed,
        out_specs=(
            P("ch", "seq"),
            P("ch", "seq"),
            P("seq", "ch"),
            P("seq", "ch"),
            P(None, "ch"),
            P("ch"),
        ),
        check_vma=False,
    )
```

```python
import jax
import jax.numpy as jnp
from jax import lax
from jax.sharding import PartitionSpec as P


def extended(cells, sides, width):
    for axis, dim in sides:
        count = lax.axis_size(axis)
        ends = count - 1
        head = lax.slice_in_dim(cells, 0, width, axis=dim)
        tail = lax.slice_in_dim(cells, cells.shape[dim] - width, cells.shape[dim], axis=dim)
        cells = jnp.concatenate(
            [
                lax.ppermute(tail, axis, [(i, (i + 1) % count) for i in range(ends)]),
                cells,
                lax.ppermute(head, axis, [((i + 1) % count, i) for i in range(ends)]),
            ],
            axis=dim,
        )
    return cells


def standardize_rows(columns_in):
    values = columns_in.astype(jnp.float32)
    average = jnp.mean(values, 0, keepdims=True)
    centred = values - average
    spread = jnp.mean(centred * centred, 0, keepdims=True)
    inverse_deviation = lax.rsqrt(spread + 1e-05)
    return (centred * inverse_deviation, inverse_deviation)


def depthwise(padded, kernel):
    channels = padded.shape[0]
    result = lax.conv_general_dilated(
        padded[None],
        kernel,
        (1,),
        "VALID",
        dimension_numbers=("NCH", "OIH", "NCH"),
        feature_group_count=channels,
        precision=lax.Precision.HIGHEST,
    )
    return result[0]


def gather_by_exchange(block, axis):
    count = lax.axis_size(axis)
    copies = jnp.broadcast_to(block[None], (count,) + block.shape)
    return lax.all_to_all(copies, axis, 0, 0, tiled=False)


def bf16_pieces(values, pieces):
    parts = []
    rest = values
    for _ in range(pieces):
        part = rest.astype(jnp.bfloat16)
        parts.append(part)
        rest = rest - part.astype(jnp.float32)
    return parts


def gather_by_shifts(block, axis):
    count = lax.axis_size(axis)
    position = lax.axis_index(axis)
    pieces = [block]
    for shift in range(1, count):
        pieces.append(
            lax.ppermute(block, axis, [(i, (i - shift) % count) for i in range(count)])
        )
    return jnp.roll(jnp.stack(pieces, 0), position, axis=0)


def reduce_by_shifts(blocks, rider, axis):
    count = lax.axis_size(axis)
    position = lax.axis_index(axis)
    total = lax.dynamic_index_in_dim(blocks, position, 0, keepdims=False).astype(jnp.float32)
    riders = rider.astype(jnp.float32)
    rows = blocks.shape[1]
    for shift in range(1, count):
        outgoing = lax.dynamic_index_in_dim(blocks, (position + shift) % count, 0, keepdims=False)
        outgoing = jnp.concatenate([outgoing, rider], 0)
        arrived = lax.ppermute(outgoing, axis, [(i, (i + shift) % count) for i in range(count)])
        total = total + arrived[:rows].astype(jnp.float32)
        riders = riders + arrived[rows:].astype(jnp.float32)
    return total, riders


def shifted_sum(padded, taps, span):
    total = taps[0][:, None] * padded[:, 0:span]
    for k in range(1, taps.shape[0]):
        total = total + taps[k][:, None] * padded[:, k : k + span]
    return total


def shards(signal, input_norm_gain, value_weight, gate_weight, depth_taps, cotangent):
    local_cols, frames = signal.shape
    groups = lax.axis_size("ch")
    blocks = lax.axis_size("seq")
    channel_position = lax.axis_index("ch")
    reach = depth_taps.shape[0] // 2
    gain_rows = jnp.stack(bf16_pieces(input_norm_gain, 3), 0)
    gain_rows = jnp.pad(gain_rows, ((0, 13), (0, frames - local_cols)))
    arrived = lax.all_gather(jnp.concatenate([signal, gain_rows], 0), "ch", axis=0)
    complete_signal = arrived[:, :local_cols].reshape(groups * local_cols, frames)
    gain_parts = arrived[:, local_cols : local_cols + 3, :local_cols].astype(jnp.float32)
    complete_gain = ((gain_parts[:, 0] + gain_parts[:, 1]) + gain_parts[:, 2]).reshape(-1)
    centered_unit, inverse_deviation = standardize_rows(complete_signal)
    normalized_signal = (centered_unit * complete_gain[:, None]).astype(jnp.bfloat16)
    centered_unit_rows = lax.dynamic_slice_in_dim(
        centered_unit, channel_position * local_cols, local_cols, 0
    )
    stacked = jnp.concatenate([value_weight, gate_weight], 1)
    gathered = gather_by_exchange(stacked, "seq").reshape(-1, stacked.shape[1])
    mixed = lax.dot_general(
        gathered, normalized_signal, (((0,), (0,)), ((), ())), preferred_element_type=jnp.float32
    )
    value = mixed[:local_cols]
    gate = mixed[local_cols:]
    sig_gate = jax.nn.sigmoid(gate)
    glued = (value * sig_gate).astype(jnp.bfloat16)
    glued_pad = extended(glued, (("seq", 1),), reach).astype(jnp.float32)
    span = glued.shape[1]
    taps_count = depth_taps.shape[0]
    pre = shifted_sum(glued_pad, depth_taps, span)
    sig_pre = jax.nn.sigmoid(pre)
    output = (pre * sig_pre).astype(jnp.bfloat16)
    grad_pre = (cotangent.astype(jnp.float32) * sig_pre * (1.0 + pre * (1.0 - sig_pre))).astype(
        jnp.bfloat16
    )
    grad_pre_f = grad_pre.astype(jnp.float32)
    grad_pad = extended(grad_pre, (("seq", 1),), reach).astype(jnp.float32)
    grad_glued = shifted_sum(grad_pad, depth_taps[::-1], span)
    tap_partial = jnp.stack(
        [jnp.sum(glued_pad[:, k : k + span] * grad_pre_f, 1) for k in range(taps_count)], 0
    )
    grad_v = (grad_glued * sig_gate).astype(jnp.bfloat16)
    grad_g = (grad_glued * value * sig_gate * (1.0 - sig_gate)).astype(jnp.bfloat16)
    grad_both = jnp.concatenate([grad_v, grad_g], 0)
    weight_partial = lax.dot_general(
        normalized_signal,
        grad_both,
        (((1,), (1,)), ((), ())),
        preferred_element_type=jnp.float32,
    )
    normed_term = jnp.dot(gathered, grad_both, preferred_element_type=jnp.float32).astype(
        jnp.bfloat16
    )
    width = weight_partial.shape[1]
    rows = value_weight.shape[0]
    taps_rows = depth_taps.shape[0]
    taps_flat = jnp.pad(tap_partial, ((0, 1), (0, 0))).reshape(blocks, -1)
    piece = taps_flat.shape[1]
    outgoing = jnp.concatenate(
        [weight_partial.astype(jnp.bfloat16).reshape(blocks, rows * width)]
        + bf16_pieces(taps_flat, 3),
        1,
    )
    arrived = lax.all_to_all(outgoing, "seq", 0, 0, tiled=False).astype(jnp.float32)
    summed = jnp.sum(arrived, 0)
    taps_summed = (
        summed[rows * width : rows * width + piece]
        + summed[rows * width + piece : rows * width + 2 * piece]
    ) + summed[rows * width + 2 * piece :]
    weight_sums = summed[: rows * width].reshape(rows, width)
    grad_value = weight_sums[:, :local_cols]
    grad_gate = weight_sums[:, local_cols:]
    normed_f = normed_term.astype(jnp.float32)
    weighted = normed_f * complete_gain[:, None]
    own_moments = jnp.stack([jnp.sum(weighted, 0), jnp.sum(weighted * centered_unit, 0)], 0)
    moment_rows = jnp.concatenate(bf16_pieces(own_moments, 3), 0)
    moment_rows = jnp.pad(moment_rows, ((0, 16 - moment_rows.shape[0]), (0, 0)))
    normalized_gradient, moment_total = reduce_by_shifts(
        normed_term.reshape(groups, local_cols, frames), moment_rows, "ch"
    )
    scaled_signal = normalized_gradient * input_norm_gain[:, None]
    moments = ((moment_total[0:2] + moment_total[2:4]) + moment_total[4:6]) * (
        1.0 / complete_signal.shape[0]
    )
    signal_gradient = (
        inverse_deviation
        * (scaled_signal - moments[0:1] - centered_unit_rows * moments[1:2])
    ).astype(jnp.bfloat16)
    gain_portion = jnp.sum(normalized_gradient * centered_unit_rows, 1)
    last = jnp.concatenate([taps_summed, gain_portion], 0)
    finished = gather_by_exchange(last, "seq")
    grad_taps = finished[:, :piece].reshape(-1)[: taps_rows * local_cols].reshape(
        taps_rows, local_cols
    )
    gain_gradient = jnp.sum(finished[:, piece:], 0)
    return (output, signal_gradient, grad_value, grad_gate, grad_taps, gain_gradient)


def solution(mesh):
    placed = (
        P("ch", "seq"),
        P("ch"),
        P("seq", "ch"),
        P("seq", "ch"),
        P(None, "ch"),
        P("ch", "seq"),
    )
    return jax.shard_map(
        shards,
        mesh=mesh,
        in_specs=placed,
        out_specs=(
            P("ch", "seq"),
            P("ch", "seq"),
            P("seq", "ch"),
            P("seq", "ch"),
            P(None, "ch"),
            P("ch"),
        ),
        check_vma=False,
    )
```

```python
import jax
import jax.numpy as jnp
from jax import lax
from jax.sharding import PartitionSpec as P


def extended(cells, sides, width):
    for axis, dim in sides:
        count = lax.axis_size(axis)
        ends = count - 1
        head = lax.slice_in_dim(cells, 0, width, axis=dim)
        tail = lax.slice_in_dim(cells, cells.shape[dim] - width, cells.shape[dim], axis=dim)
        cells = jnp.concatenate(
            [
                lax.ppermute(tail, axis, [(i, (i + 1) % count) for i in range(ends)]),
                cells,
                lax.ppermute(head, axis, [((i + 1) % count, i) for i in range(ends)]),
            ],
            axis=dim,
        )
    return cells


def standardize_rows(columns_in):
    values = columns_in.astype(jnp.float32)
    average = jnp.mean(values, 0, keepdims=True)
    centred = values - average
    spread = jnp.mean(centred * centred, 0, keepdims=True)
    inverse_deviation = lax.rsqrt(spread + 1e-05)
    return (centred * inverse_deviation, inverse_deviation)


def depthwise(padded, kernel):
    channels = padded.shape[0]
    result = lax.conv_general_dilated(
        padded[None],
        kernel,
        (1,),
        "VALID",
        dimension_numbers=("NCH", "OIH", "NCH"),
        feature_group_count=channels,
        precision=lax.Precision.HIGHEST,
    )
    return result[0]


def gather_by_exchange(block, axis):
    count = lax.axis_size(axis)
    copies = jnp.broadcast_to(block[None], (count,) + block.shape)
    return lax.all_to_all(copies, axis, 0, 0, tiled=False)


def bf16_pieces(values, pieces):
    parts = []
    rest = values
    for _ in range(pieces):
        part = rest.astype(jnp.bfloat16)
        parts.append(part)
        rest = rest - part.astype(jnp.float32)
    return parts


def gather_by_shifts(block, axis):
    count = lax.axis_size(axis)
    position = lax.axis_index(axis)
    pieces = [block]
    for shift in range(1, count):
        pieces.append(
            lax.ppermute(block, axis, [(i, (i - shift) % count) for i in range(count)])
        )
    return jnp.roll(jnp.stack(pieces, 0), position, axis=0)


def reduce_by_shifts(blocks, rider, axis):
    count = lax.axis_size(axis)
    position = lax.axis_index(axis)
    total = lax.dynamic_index_in_dim(blocks, position, 0, keepdims=False).astype(jnp.float32)
    riders = rider.astype(jnp.float32)
    rows = blocks.shape[1]
    for shift in range(1, count):
        outgoing = lax.dynamic_index_in_dim(blocks, (position + shift) % count, 0, keepdims=False)
        outgoing = jnp.concatenate([outgoing, rider], 0)
        arrived = lax.ppermute(outgoing, axis, [(i, (i + shift) % count) for i in range(count)])
        total = total + arrived[:rows].astype(jnp.float32)
        riders = riders + arrived[rows:].astype(jnp.float32)
    return total, riders


def shifted_sum(padded, taps, span):
    total = taps[0][:, None] * padded[:, 0:span]
    for k in range(1, taps.shape[0]):
        total = total + taps[k][:, None] * padded[:, k : k + span]
    return total


def shards(signal, input_norm_gain, value_weight, gate_weight, depth_taps, cotangent):
    local_cols, frames = signal.shape
    groups = lax.axis_size("ch")
    blocks = lax.axis_size("seq")
    channel_position = lax.axis_index("ch")
    reach = depth_taps.shape[0] // 2
    gain_rows = jnp.stack(bf16_pieces(input_norm_gain, 3), 0)
    gain_rows = jnp.pad(gain_rows, ((0, 13), (0, frames - local_cols)))
    arrived = lax.all_gather(jnp.concatenate([signal, gain_rows], 0), "ch", axis=0)
    complete_signal = arrived[:, :local_cols].reshape(groups * local_cols, frames)
    gain_parts = arrived[:, local_cols : local_cols + 3, :local_cols].astype(jnp.float32)
    complete_gain = ((gain_parts[:, 0] + gain_parts[:, 1]) + gain_parts[:, 2]).reshape(-1)
    centered_unit, inverse_deviation = standardize_rows(complete_signal)
    normalized_signal = (centered_unit * complete_gain[:, None]).astype(jnp.bfloat16)
    centered_unit_rows = lax.dynamic_slice_in_dim(
        centered_unit, channel_position * local_cols, local_cols, 0
    )
    stacked = jnp.concatenate([value_weight, gate_weight], 1)
    gathered = gather_by_exchange(stacked, "seq").reshape(-1, stacked.shape[1])
    mixed = lax.dot_general(
        gathered, normalized_signal, (((0,), (0,)), ((), ())), preferred_element_type=jnp.float32
    )
    value = mixed[:local_cols]
    gate = mixed[local_cols:]
    sig_gate = jax.nn.sigmoid(gate)
    glued = (value * sig_gate).astype(jnp.bfloat16)
    glued_pad = extended(glued, (("seq", 1),), reach).astype(jnp.float32)
    span = glued.shape[1]
    taps_count = depth_taps.shape[0]
    pre = shifted_sum(glued_pad, depth_taps, span)
    sig_pre = jax.nn.sigmoid(pre)
    output = (pre * sig_pre).astype(jnp.bfloat16)
    grad_pre = (cotangent.astype(jnp.float32) * sig_pre * (1.0 + pre * (1.0 - sig_pre))).astype(
        jnp.bfloat16
    )
    grad_pre_f = grad_pre.astype(jnp.float32)
    grad_pad = extended(grad_pre, (("seq", 1),), reach).astype(jnp.float32)
    grad_glued = shifted_sum(grad_pad, depth_taps[::-1], span)
    tap_partial = jnp.stack(
        [jnp.sum(glued_pad[:, k : k + span] * grad_pre_f, 1) for k in range(taps_count)], 0
    )
    grad_v = (grad_glued * sig_gate).astype(jnp.bfloat16)
    grad_g = (grad_glued * value * sig_gate * (1.0 - sig_gate)).astype(jnp.bfloat16)
    grad_both = jnp.concatenate([grad_v, grad_g], 0)
    weight_partial = lax.dot_general(
        normalized_signal,
        grad_both,
        (((1,), (1,)), ((), ())),
        preferred_element_type=jnp.float32,
    )
    normed_term = jnp.dot(gathered, grad_both, preferred_element_type=jnp.float32).astype(
        jnp.bfloat16
    )
    width = weight_partial.shape[1]
    rows = value_weight.shape[0]
    taps_rows = depth_taps.shape[0]
    taps_flat = jnp.pad(tap_partial, ((0, 1), (0, 0))).reshape(blocks, -1)
    piece = taps_flat.shape[1]
    outgoing = jnp.concatenate([weight_partial.reshape(blocks, rows * width), taps_flat], 1)
    summed = jnp.sum(lax.all_to_all(outgoing, "seq", 0, 0, tiled=False), 0)
    weight_sums = summed[: rows * width].reshape(rows, width)
    grad_value = weight_sums[:, :local_cols]
    grad_gate = weight_sums[:, local_cols:]
    normed_f = normed_term.astype(jnp.float32)
    weighted = normed_f * complete_gain[:, None]
    own_moments = jnp.stack([jnp.sum(weighted, 0), jnp.sum(weighted * centered_unit, 0)], 0)
    moment_rows = jnp.concatenate(bf16_pieces(own_moments, 3), 0)
    moment_rows = jnp.pad(moment_rows, ((0, 16 - moment_rows.shape[0]), (0, 0)))
    normalized_gradient, moment_total = reduce_by_shifts(
        normed_term.reshape(groups, local_cols, frames), moment_rows, "ch"
    )
    scaled_signal = normalized_gradient * input_norm_gain[:, None]
    moments = ((moment_total[0:2] + moment_total[2:4]) + moment_total[4:6]) * (
        1.0 / complete_signal.shape[0]
    )
    signal_gradient = (
        inverse_deviation
        * (scaled_signal - moments[0:1] - centered_unit_rows * moments[1:2])
    ).astype(jnp.bfloat16)
    gain_portion = jnp.sum(normalized_gradient * centered_unit_rows, 1)
    last = jnp.concatenate([summed[rows * width :], gain_portion], 0)
    finished = lax.all_gather(last, "seq", axis=0)
    grad_taps = finished[:, :piece].reshape(-1)[: taps_rows * local_cols].reshape(
        taps_rows, local_cols
    )
    gain_gradient = jnp.sum(finished[:, piece:], 0)
    return (output, signal_gradient, grad_value, grad_gate, grad_taps, gain_gradient)


def solution(mesh):
    placed = (
        P("ch", "seq"),
        P("ch"),
        P("seq", "ch"),
        P("seq", "ch"),
        P(None, "ch"),
        P("ch", "seq"),
    )
    return jax.shard_map(
        shards,
        mesh=mesh,
        in_specs=placed,
        out_specs=(
            P("ch", "seq"),
            P("ch", "seq"),
            P("seq", "ch"),
            P("seq", "ch"),
            P(None, "ch"),
            P("ch"),
        ),
        check_vma=False,
    )
```

```python
import jax
import jax.numpy as jnp
from jax import lax
from jax.sharding import PartitionSpec as P


def extended(cells, sides, width):
    for axis, dim in sides:
        count = lax.axis_size(axis)
        ends = count - 1
        head = lax.slice_in_dim(cells, 0, width, axis=dim)
        tail = lax.slice_in_dim(cells, cells.shape[dim] - width, cells.shape[dim], axis=dim)
        cells = jnp.concatenate(
            [
                lax.ppermute(tail, axis, [(i, (i + 1) % count) for i in range(ends)]),
                cells,
                lax.ppermute(head, axis, [((i + 1) % count, i) for i in range(ends)]),
            ],
            axis=dim,
        )
    return cells


def standardize_rows(columns_in):
    values = columns_in.astype(jnp.float32)
    average = jnp.mean(values, 0, keepdims=True)
    centred = values - average
    spread = jnp.mean(centred * centred, 0, keepdims=True)
    inverse_deviation = lax.rsqrt(spread + 1e-05)
    return (centred * inverse_deviation, inverse_deviation)


def depthwise(padded, kernel):
    channels = padded.shape[0]
    result = lax.conv_general_dilated(
        padded[None],
        kernel,
        (1,),
        "VALID",
        dimension_numbers=("NCH", "OIH", "NCH"),
        feature_group_count=channels,
        precision=lax.Precision.HIGHEST,
    )
    return result[0]


def gather_by_exchange(block, axis):
    count = lax.axis_size(axis)
    copies = jnp.broadcast_to(block[None], (count,) + block.shape)
    return lax.all_to_all(copies, axis, 0, 0, tiled=False)


def bf16_pieces(values, pieces):
    parts = []
    rest = values
    for _ in range(pieces):
        part = rest.astype(jnp.bfloat16)
        parts.append(part)
        rest = rest - part.astype(jnp.float32)
    return parts


def gather_by_shifts(block, axis):
    count = lax.axis_size(axis)
    position = lax.axis_index(axis)
    pieces = [block]
    for shift in range(1, count):
        pieces.append(
            lax.ppermute(block, axis, [(i, (i - shift) % count) for i in range(count)])
        )
    return jnp.roll(jnp.stack(pieces, 0), position, axis=0)


def reduce_by_shifts(blocks, rider, axis):
    count = lax.axis_size(axis)
    position = lax.axis_index(axis)
    total = lax.dynamic_index_in_dim(blocks, position, 0, keepdims=False).astype(jnp.float32)
    riders = rider.astype(jnp.float32)
    rows = blocks.shape[1]
    for shift in range(1, count):
        outgoing = lax.dynamic_index_in_dim(blocks, (position + shift) % count, 0, keepdims=False)
        outgoing = jnp.concatenate([outgoing, rider], 0)
        arrived = lax.ppermute(outgoing, axis, [(i, (i + shift) % count) for i in range(count)])
        total = total + arrived[:rows].astype(jnp.float32)
        riders = riders + arrived[rows:].astype(jnp.float32)
    return total, riders


def shifted_sum(padded, taps, span):
    total = taps[0][:, None] * padded[:, 0:span]
    for k in range(1, taps.shape[0]):
        total = total + taps[k][:, None] * padded[:, k : k + span]
    return total


def shards(signal, input_norm_gain, value_weight, gate_weight, depth_taps, cotangent):
    local_cols, frames = signal.shape
    groups = lax.axis_size("ch")
    blocks = lax.axis_size("seq")
    channel_position = lax.axis_index("ch")
    reach = depth_taps.shape[0] // 2
    gain_rows = jnp.stack(bf16_pieces(input_norm_gain, 3), 0)
    gain_rows = jnp.pad(gain_rows, ((0, 13), (0, frames - local_cols)))
    arrived = lax.all_gather(jnp.concatenate([signal, gain_rows], 0), "ch", axis=0)
    complete_signal = arrived[:, :local_cols].reshape(groups * local_cols, frames)
    gain_parts = arrived[:, local_cols : local_cols + 3, :local_cols].astype(jnp.float32)
    complete_gain = ((gain_parts[:, 0] + gain_parts[:, 1]) + gain_parts[:, 2]).reshape(-1)
    centered_unit, inverse_deviation = standardize_rows(complete_signal)
    normalized_signal = (centered_unit * complete_gain[:, None]).astype(jnp.bfloat16)
    centered_unit_rows = lax.dynamic_slice_in_dim(
        centered_unit, channel_position * local_cols, local_cols, 0
    )
    stacked = jnp.concatenate([value_weight, gate_weight], 1)
    gathered = gather_by_exchange(stacked, "seq").reshape(-1, stacked.shape[1])
    mixed = lax.dot_general(
        gathered, normalized_signal, (((0,), (0,)), ((), ())), preferred_element_type=jnp.float32
    )
    value = mixed[:local_cols]
    gate = mixed[local_cols:]
    sig_gate = jax.nn.sigmoid(gate)
    glued = (value * sig_gate).astype(jnp.bfloat16)
    glued_pad = extended(glued, (("seq", 1),), reach).astype(jnp.float32)
    span = glued.shape[1]
    taps_count = depth_taps.shape[0]
    pre = shifted_sum(glued_pad, depth_taps, span)
    sig_pre = jax.nn.sigmoid(pre)
    output = (pre * sig_pre).astype(jnp.bfloat16)
    grad_pre = (cotangent.astype(jnp.float32) * sig_pre * (1.0 + pre * (1.0 - sig_pre))).astype(
        jnp.bfloat16
    )
    grad_pre_f = grad_pre.astype(jnp.float32)
    grad_pad = extended(grad_pre, (("seq", 1),), reach).astype(jnp.float32)
    grad_glued = shifted_sum(grad_pad, depth_taps[::-1], span)
    tap_partial = jnp.stack(
        [jnp.sum(glued_pad[:, k : k + span] * grad_pre_f, 1) for k in range(taps_count)], 0
    )
    grad_v = (grad_glued * sig_gate).astype(jnp.bfloat16)
    grad_g = (grad_glued * value * sig_gate * (1.0 - sig_gate)).astype(jnp.bfloat16)
    grad_both = jnp.concatenate([grad_v, grad_g], 0)
    weight_partial = lax.dot_general(
        normalized_signal,
        grad_both,
        (((1,), (1,)), ((), ())),
        preferred_element_type=jnp.float32,
    )
    normed_term = jnp.dot(gathered, grad_both, preferred_element_type=jnp.float32).astype(
        jnp.bfloat16
    )
    width = weight_partial.shape[1]
    rows = value_weight.shape[0]
    taps_rows = depth_taps.shape[0]
    taps_flat = jnp.pad(tap_partial, ((0, 1), (0, 0))).reshape(blocks, -1)
    piece = taps_flat.shape[1]
    taps_row = jnp.concatenate(bf16_pieces(taps_flat, 3), 1)
    taps_row = jnp.pad(taps_row, ((0, 0), (0, width - taps_row.shape[1])))
    outgoing = jnp.concatenate(
        [weight_partial.astype(jnp.bfloat16).reshape(blocks, rows, width), taps_row[:, None]], 1
    )
    summed = jnp.sum(lax.all_to_all(outgoing, "seq", 0, 0, tiled=False).astype(jnp.float32), 0)
    weight_sums = summed[:rows]
    taps_summed = (summed[rows, :piece] + summed[rows, piece : 2 * piece]) + summed[
        rows, 2 * piece : 3 * piece
    ]
    grad_value = weight_sums[:, :local_cols]
    grad_gate = weight_sums[:, local_cols:]
    normed_f = normed_term.astype(jnp.float32)
    weighted = normed_f * complete_gain[:, None]
    own_moments = jnp.stack([jnp.sum(weighted, 0), jnp.sum(weighted * centered_unit, 0)], 0)
    moment_rows = jnp.concatenate(bf16_pieces(own_moments, 3), 0)
    half = frames // 2
    moment_rows = moment_rows.reshape(-1, half)
    moment_rows = jnp.pad(moment_rows, ((0, 16 - moment_rows.shape[0]), (0, 0)))
    early_part = lax.psum_scatter(
        normed_term[:, :half].astype(jnp.float32), "ch", scatter_dimension=0, tiled=True
    )
    late_part, moment_total = reduce_by_shifts(
        normed_term[:, half:].reshape(groups, local_cols, frames - half), moment_rows, "ch"
    )
    normalized_gradient = jnp.concatenate([early_part, late_part], 1)
    moment_total = moment_total[:12].reshape(6, frames)
    scaled_signal = normalized_gradient * input_norm_gain[:, None]
    moments = ((moment_total[0:2] + moment_total[2:4]) + moment_total[4:6]) * (
        1.0 / complete_signal.shape[0]
    )
    signal_gradient = (
        inverse_deviation
        * (scaled_signal - moments[0:1] - centered_unit_rows * moments[1:2])
    ).astype(jnp.bfloat16)
    gain_portion = jnp.sum(normalized_gradient * centered_unit_rows, 1)
    last = jnp.concatenate([taps_summed, gain_portion], 0)
    finished = gather_by_exchange(last, "seq")
    grad_taps = finished[:, :piece].reshape(-1)[: taps_rows * local_cols].reshape(
        taps_rows, local_cols
    )
    gain_gradient = jnp.sum(finished[:, piece:], 0)
    return (output, signal_gradient, grad_value, grad_gate, grad_taps, gain_gradient)


def solution(mesh):
    placed = (
        P("ch", "seq"),
        P("ch"),
        P("seq", "ch"),
        P("seq", "ch"),
        P(None, "ch"),
        P("ch", "seq"),
    )
    return jax.shard_map(
        shards,
        mesh=mesh,
        in_specs=placed,
        out_specs=(
            P("ch", "seq"),
            P("ch", "seq"),
            P("seq", "ch"),
            P("seq", "ch"),
            P(None, "ch"),
            P("ch"),
        ),
        check_vma=False,
    )
```

```python
import jax
import jax.numpy as jnp
from jax import lax
from jax.sharding import PartitionSpec as P


def extended(cells, sides, width):
    for axis, dim in sides:
        count = lax.axis_size(axis)
        ends = count - 1
        head = lax.slice_in_dim(cells, 0, width, axis=dim)
        tail = lax.slice_in_dim(cells, cells.shape[dim] - width, cells.shape[dim], axis=dim)
        cells = jnp.concatenate(
            [
                lax.ppermute(tail, axis, [(i, (i + 1) % count) for i in range(ends)]),
                cells,
                lax.ppermute(head, axis, [((i + 1) % count, i) for i in range(ends)]),
            ],
            axis=dim,
        )
    return cells


def standardize_rows(columns_in):
    values = columns_in.astype(jnp.float32)
    average = jnp.mean(values, 0, keepdims=True)
    centred = values - average
    spread = jnp.mean(centred * centred, 0, keepdims=True)
    inverse_deviation = lax.rsqrt(spread + 1e-05)
    return (centred * inverse_deviation, inverse_deviation)


def depthwise(padded, kernel):
    channels = padded.shape[0]
    result = lax.conv_general_dilated(
        padded[None],
        kernel,
        (1,),
        "VALID",
        dimension_numbers=("NCH", "OIH", "NCH"),
        feature_group_count=channels,
        precision=lax.Precision.HIGHEST,
    )
    return result[0]


def gather_by_exchange(block, axis):
    count = lax.axis_size(axis)
    copies = jnp.broadcast_to(block[None], (count,) + block.shape)
    return lax.all_to_all(copies, axis, 0, 0, tiled=False)


def bf16_pieces(values, pieces):
    parts = []
    rest = values
    for _ in range(pieces):
        part = rest.astype(jnp.bfloat16)
        parts.append(part)
        rest = rest - part.astype(jnp.float32)
    return parts


def gather_by_shifts(block, axis):
    count = lax.axis_size(axis)
    position = lax.axis_index(axis)
    pieces = [block]
    for shift in range(1, count):
        pieces.append(
            lax.ppermute(block, axis, [(i, (i - shift) % count) for i in range(count)])
        )
    return jnp.roll(jnp.stack(pieces, 0), position, axis=0)


def reduce_by_shifts(blocks, rider, axis):
    count = lax.axis_size(axis)
    position = lax.axis_index(axis)
    total = lax.dynamic_index_in_dim(blocks, position, 0, keepdims=False).astype(jnp.float32)
    riders = rider.astype(jnp.float32)
    rows = blocks.shape[1]
    for shift in range(1, count):
        outgoing = lax.dynamic_index_in_dim(blocks, (position + shift) % count, 0, keepdims=False)
        outgoing = jnp.concatenate([outgoing, rider], 0)
        arrived = lax.ppermute(outgoing, axis, [(i, (i + shift) % count) for i in range(count)])
        total = total + arrived[:rows].astype(jnp.float32)
        riders = riders + arrived[rows:].astype(jnp.float32)
    return total, riders


def shifted_sum(padded, taps, span):
    total = taps[0][:, None] * padded[:, 0:span]
    for k in range(1, taps.shape[0]):
        total = total + taps[k][:, None] * padded[:, k : k + span]
    return total


def shards(signal, input_norm_gain, value_weight, gate_weight, depth_taps, cotangent):
    local_cols, frames = signal.shape
    groups = lax.axis_size("ch")
    blocks = lax.axis_size("seq")
    channel_position = lax.axis_index("ch")
    reach = depth_taps.shape[0] // 2
    gain_rows = jnp.stack(bf16_pieces(input_norm_gain, 3), 0)
    half = frames // 2
    gain_rows = jnp.pad(gain_rows, ((0, 13), (0, half - local_cols)))
    arrived = lax.all_gather(jnp.concatenate([signal[:, :half], gain_rows], 0), "ch", axis=0)
    arrived_late = gather_by_shifts(signal[:, half:], "ch")
    complete_signal = jnp.concatenate([arrived[:, :local_cols], arrived_late], 2).reshape(
        groups * local_cols, frames
    )
    gain_parts = arrived[:, local_cols : local_cols + 3, :local_cols].astype(jnp.float32)
    complete_gain = ((gain_parts[:, 0] + gain_parts[:, 1]) + gain_parts[:, 2]).reshape(-1)
    centered_unit, inverse_deviation = standardize_rows(complete_signal)
    normalized_signal = (centered_unit * complete_gain[:, None]).astype(jnp.bfloat16)
    centered_unit_rows = lax.dynamic_slice_in_dim(
        centered_unit, channel_position * local_cols, local_cols, 0
    )
    stacked = jnp.concatenate([value_weight, gate_weight], 1)
    gathered = gather_by_exchange(stacked, "seq").reshape(-1, stacked.shape[1])
    mixed = lax.dot_general(
        gathered, normalized_signal, (((0,), (0,)), ((), ())), preferred_element_type=jnp.float32
    )
    value = mixed[:local_cols]
    gate = mixed[local_cols:]
    sig_gate = jax.nn.sigmoid(gate)
    glued = (value * sig_gate).astype(jnp.bfloat16)
    glued_pad = extended(glued, (("seq", 1),), reach).astype(jnp.float32)
    span = glued.shape[1]
    taps_count = depth_taps.shape[0]
    pre = shifted_sum(glued_pad, depth_taps, span)
    sig_pre = jax.nn.sigmoid(pre)
    output = (pre * sig_pre).astype(jnp.bfloat16)
    grad_pre = (cotangent.astype(jnp.float32) * sig_pre * (1.0 + pre * (1.0 - sig_pre))).astype(
        jnp.bfloat16
    )
    grad_pre_f = grad_pre.astype(jnp.float32)
    grad_pad = extended(grad_pre, (("seq", 1),), reach).astype(jnp.float32)
    grad_glued = shifted_sum(grad_pad, depth_taps[::-1], span)
    tap_partial = jnp.stack(
        [jnp.sum(glued_pad[:, k : k + span] * grad_pre_f, 1) for k in range(taps_count)], 0
    )
    grad_v = (grad_glued * sig_gate).astype(jnp.bfloat16)
    grad_g = (grad_glued * value * sig_gate * (1.0 - sig_gate)).astype(jnp.bfloat16)
    grad_both = jnp.concatenate([grad_v, grad_g], 0)
    weight_partial = lax.dot_general(
        normalized_signal,
        grad_both,
        (((1,), (1,)), ((), ())),
        preferred_element_type=jnp.float32,
    )
    normed_term = jnp.dot(gathered, grad_both, preferred_element_type=jnp.float32).astype(
        jnp.bfloat16
    )
    width = weight_partial.shape[1]
    rows = value_weight.shape[0]
    taps_rows = depth_taps.shape[0]
    taps_flat = jnp.pad(tap_partial, ((0, 1), (0, 0))).reshape(blocks, -1)
    piece = taps_flat.shape[1]
    taps_row = jnp.concatenate(bf16_pieces(taps_flat, 3), 1)
    taps_row = jnp.pad(taps_row, ((0, 0), (0, width - taps_row.shape[1])))
    outgoing = jnp.concatenate(
        [weight_partial.astype(jnp.bfloat16).reshape(blocks, rows, width), taps_row[:, None]], 1
    )
    summed = jnp.sum(lax.all_to_all(outgoing, "seq", 0, 0, tiled=False).astype(jnp.float32), 0)
    weight_sums = summed[:rows]
    taps_summed = (summed[rows, :piece] + summed[rows, piece : 2 * piece]) + summed[
        rows, 2 * piece : 3 * piece
    ]
    grad_value = weight_sums[:, :local_cols]
    grad_gate = weight_sums[:, local_cols:]
    normed_f = normed_term.astype(jnp.float32)
    weighted = normed_f * complete_gain[:, None]
    own_moments = jnp.stack([jnp.sum(weighted, 0), jnp.sum(weighted * centered_unit, 0)], 0)
    moment_rows = jnp.concatenate(bf16_pieces(own_moments, 3), 0)
    moment_rows = moment_rows.reshape(-1, half)
    moment_rows = jnp.pad(moment_rows, ((0, 16 - moment_rows.shape[0]), (0, 0)))
    early_part = lax.psum_scatter(
        normed_term[:, :half].astype(jnp.float32), "ch", scatter_dimension=0, tiled=True
    )
    late_part, moment_total = reduce_by_shifts(
        normed_term[:, half:].reshape(groups, local_cols, frames - half), moment_rows, "ch"
    )
    normalized_gradient = jnp.concatenate([early_part, late_part], 1)
    moment_total = moment_total[:12].reshape(6, frames)
    scaled_signal = normalized_gradient * input_norm_gain[:, None]
    moments = ((moment_total[0:2] + moment_total[2:4]) + moment_total[4:6]) * (
        1.0 / complete_signal.shape[0]
    )
    signal_gradient = (
        inverse_deviation
        * (scaled_signal - moments[0:1] - centered_unit_rows * moments[1:2])
    ).astype(jnp.bfloat16)
    gain_portion = jnp.sum(normalized_gradient * centered_unit_rows, 1)
    last = jnp.concatenate([taps_summed, gain_portion], 0)
    finished = gather_by_exchange(last, "seq")
    grad_taps = finished[:, :piece].reshape(-1)[: taps_rows * local_cols].reshape(
        taps_rows, local_cols
    )
    gain_gradient = jnp.sum(finished[:, piece:], 0)
    return (output, signal_gradient, grad_value, grad_gate, grad_taps, gain_gradient)


def solution(mesh):
    placed = (
        P("ch", "seq"),
        P("ch"),
        P("seq", "ch"),
        P("seq", "ch"),
        P(None, "ch"),
        P("ch", "seq"),
    )
    return jax.shard_map(
        shards,
        mesh=mesh,
        in_specs=placed,
        out_specs=(
            P("ch", "seq"),
            P("ch", "seq"),
            P("seq", "ch"),
            P("seq", "ch"),
            P(None, "ch"),
            P("ch"),
        ),
        check_vma=False,
    )
```

```python
import jax
import jax.numpy as jnp
from jax import lax
from jax.sharding import PartitionSpec as P


def extended(cells, sides, width):
    for axis, dim in sides:
        count = lax.axis_size(axis)
        ends = count - 1
        head = lax.slice_in_dim(cells, 0, width, axis=dim)
        tail = lax.slice_in_dim(cells, cells.shape[dim] - width, cells.shape[dim], axis=dim)
        cells = jnp.concatenate(
            [
                lax.ppermute(tail, axis, [(i, (i + 1) % count) for i in range(ends)]),
                cells,
                lax.ppermute(head, axis, [((i + 1) % count, i) for i in range(ends)]),
            ],
            axis=dim,
        )
    return cells


def standardize_rows(columns_in):
    values = columns_in.astype(jnp.float32)
    average = jnp.mean(values, 0, keepdims=True)
    centred = values - average
    spread = jnp.mean(centred * centred, 0, keepdims=True)
    inverse_deviation = lax.rsqrt(spread + 1e-05)
    return (centred * inverse_deviation, inverse_deviation)


def depthwise(padded, kernel):
    channels = padded.shape[0]
    result = lax.conv_general_dilated(
        padded[None],
        kernel,
        (1,),
        "VALID",
        dimension_numbers=("NCH", "OIH", "NCH"),
        feature_group_count=channels,
        precision=lax.Precision.HIGHEST,
    )
    return result[0]


def gather_by_exchange(block, axis):
    count = lax.axis_size(axis)
    copies = jnp.broadcast_to(block[None], (count,) + block.shape)
    return lax.all_to_all(copies, axis, 0, 0, tiled=False)


def bf16_pieces(values, pieces):
    parts = []
    rest = values
    for _ in range(pieces):
        part = rest.astype(jnp.bfloat16)
        parts.append(part)
        rest = rest - part.astype(jnp.float32)
    return parts


def gather_by_shifts(block, axis):
    count = lax.axis_size(axis)
    position = lax.axis_index(axis)
    pieces = [block]
    for shift in range(1, count):
        pieces.append(
            lax.ppermute(block, axis, [(i, (i - shift) % count) for i in range(count)])
        )
    return jnp.roll(jnp.stack(pieces, 0), position, axis=0)


def reduce_by_shifts(blocks, rider, axis):
    count = lax.axis_size(axis)
    position = lax.axis_index(axis)
    total = lax.dynamic_index_in_dim(blocks, position, 0, keepdims=False).astype(jnp.float32)
    riders = rider.astype(jnp.float32)
    rows = blocks.shape[1]
    for shift in range(1, count):
        outgoing = lax.dynamic_index_in_dim(blocks, (position + shift) % count, 0, keepdims=False)
        outgoing = jnp.concatenate([outgoing, rider], 0)
        arrived = lax.ppermute(outgoing, axis, [(i, (i + shift) % count) for i in range(count)])
        total = total + arrived[:rows].astype(jnp.float32)
        riders = riders + arrived[rows:].astype(jnp.float32)
    return total, riders


def shifted_sum(padded, taps, span):
    total = taps[0][:, None] * padded[:, 0:span]
    for k in range(1, taps.shape[0]):
        total = total + taps[k][:, None] * padded[:, k : k + span]
    return total


def shards(signal, input_norm_gain, value_weight, gate_weight, depth_taps, cotangent):
    local_cols, frames = signal.shape
    groups = lax.axis_size("ch")
    blocks = lax.axis_size("seq")
    channel_position = lax.axis_index("ch")
    reach = depth_taps.shape[0] // 2
    span = frames
    cotangent_wide = extended(cotangent, (("seq", 1),), reach)
    gain_rows = jnp.stack(bf16_pieces(input_norm_gain, 3), 0)
    gain_rows = jnp.pad(gain_rows, ((0, 13), (0, frames - local_cols)))
    arrived = lax.all_gather(jnp.concatenate([signal, gain_rows], 0), "ch", axis=0)
    complete_signal = arrived[:, :local_cols].reshape(groups * local_cols, frames)
    gain_parts = arrived[:, local_cols : local_cols + 3, :local_cols].astype(jnp.float32)
    complete_gain = ((gain_parts[:, 0] + gain_parts[:, 1]) + gain_parts[:, 2]).reshape(-1)
    centered_unit, inverse_deviation = standardize_rows(complete_signal)
    normalized_signal = (centered_unit * complete_gain[:, None]).astype(jnp.bfloat16)
    centered_unit_rows = lax.dynamic_slice_in_dim(
        centered_unit, channel_position * local_cols, local_cols, 0
    )
    stacked = jnp.concatenate([value_weight, gate_weight], 1)
    gathered = gather_by_exchange(stacked, "seq").reshape(-1, stacked.shape[1])
    mixed = lax.dot_general(
        gathered, normalized_signal, (((0,), (0,)), ((), ())), preferred_element_type=jnp.float32
    )
    value = mixed[:local_cols]
    gate = mixed[local_cols:]
    sig_gate = jax.nn.sigmoid(gate)
    glued = (value * sig_gate).astype(jnp.bfloat16)
    glued_wide = extended(glued, (("seq", 1),), 2 * reach).astype(jnp.float32)
    glued_pad = glued_wide[:, reach : reach + span + 2 * reach]
    taps_count = depth_taps.shape[0]
    pre_wide = shifted_sum(glued_wide, depth_taps, span + 2 * reach)
    sig_pre_wide = jax.nn.sigmoid(pre_wide)
    pre = pre_wide[:, reach : reach + span]
    sig_pre = sig_pre_wide[:, reach : reach + span]
    output = (pre * sig_pre).astype(jnp.bfloat16)
    grad_pad = (
        cotangent_wide.astype(jnp.float32)
        * sig_pre_wide
        * (1.0 + pre_wide * (1.0 - sig_pre_wide))
    ).astype(jnp.bfloat16)
    grad_pre_f = grad_pad[:, reach : reach + span].astype(jnp.float32)
    grad_glued = shifted_sum(grad_pad.astype(jnp.float32), depth_taps[::-1], span)
    tap_partial = jnp.stack(
        [jnp.sum(glued_pad[:, k : k + span] * grad_pre_f, 1) for k in range(taps_count)], 0
    )
    grad_v = (grad_glued * sig_gate).astype(jnp.bfloat16)
    grad_g = (grad_glued * value * sig_gate * (1.0 - sig_gate)).astype(jnp.bfloat16)
    grad_both = jnp.concatenate([grad_v, grad_g], 0)
    weight_partial = lax.dot_general(
        normalized_signal,
        grad_both,
        (((1,), (1,)), ((), ())),
        preferred_element_type=jnp.float32,
    )
    normed_term = jnp.dot(gathered, grad_both, preferred_element_type=jnp.float32).astype(
        jnp.bfloat16
    )
    width = weight_partial.shape[1]
    rows = value_weight.shape[0]
    taps_rows = depth_taps.shape[0]
    taps_flat = jnp.pad(tap_partial, ((0, 1), (0, 0))).reshape(blocks, -1)
    piece = taps_flat.shape[1]
    taps_row = jnp.concatenate(bf16_pieces(taps_flat, 3), 1)
    taps_row = jnp.pad(taps_row, ((0, 0), (0, width - taps_row.shape[1])))
    outgoing = jnp.concatenate(
        [weight_partial.astype(jnp.bfloat16).reshape(blocks, rows, width), taps_row[:, None]], 1
    )
    summed = jnp.sum(lax.all_to_all(outgoing, "seq", 0, 0, tiled=False).astype(jnp.float32), 0)
    weight_sums = summed[:rows]
    taps_summed = (summed[rows, :piece] + summed[rows, piece : 2 * piece]) + summed[
        rows, 2 * piece : 3 * piece
    ]
    grad_value = weight_sums[:, :local_cols]
    grad_gate = weight_sums[:, local_cols:]
    normed_f = normed_term.astype(jnp.float32)
    weighted = normed_f * complete_gain[:, None]
    own_moments = jnp.stack([jnp.sum(weighted, 0), jnp.sum(weighted * centered_unit, 0)], 0)
    moment_rows = jnp.concatenate(bf16_pieces(own_moments, 3), 0)
    half = frames // 2
    moment_rows = moment_rows.reshape(-1, half)
    moment_rows = jnp.pad(moment_rows, ((0, 16 - moment_rows.shape[0]), (0, 0)))
    early_part = lax.psum_scatter(
        normed_term[:, :half].astype(jnp.float32), "ch", scatter_dimension=0, tiled=True
    )
    late_part, moment_total = reduce_by_shifts(
        normed_term[:, half:].reshape(groups, local_cols, frames - half), moment_rows, "ch"
    )
    normalized_gradient = jnp.concatenate([early_part, late_part], 1)
    moment_total = moment_total[:12].reshape(6, frames)
    scaled_signal = normalized_gradient * input_norm_gain[:, None]
    moments = ((moment_total[0:2] + moment_total[2:4]) + moment_total[4:6]) * (
        1.0 / complete_signal.shape[0]
    )
    signal_gradient = (
        inverse_deviation
        * (scaled_signal - moments[0:1] - centered_unit_rows * moments[1:2])
    ).astype(jnp.bfloat16)
    gain_portion = jnp.sum(normalized_gradient * centered_unit_rows, 1)
    last = jnp.concatenate([taps_summed, gain_portion], 0)
    finished = gather_by_exchange(last, "seq")
    grad_taps = finished[:, :piece].reshape(-1)[: taps_rows * local_cols].reshape(
        taps_rows, local_cols
    )
    gain_gradient = jnp.sum(finished[:, piece:], 0)
    return (output, signal_gradient, grad_value, grad_gate, grad_taps, gain_gradient)


def solution(mesh):
    placed = (
        P("ch", "seq"),
        P("ch"),
        P("seq", "ch"),
        P("seq", "ch"),
        P(None, "ch"),
        P("ch", "seq"),
    )
    return jax.shard_map(
        shards,
        mesh=mesh,
        in_specs=placed,
        out_specs=(
            P("ch", "seq"),
            P("ch", "seq"),
            P("seq", "ch"),
            P("seq", "ch"),
            P(None, "ch"),
            P("ch"),
        ),
        check_vma=False,
    )
```

```python
import jax
import jax.numpy as jnp
from jax import lax
from jax.sharding import PartitionSpec as P


def extended(cells, sides, width):
    for axis, dim in sides:
        count = lax.axis_size(axis)
        ends = count - 1
        head = lax.slice_in_dim(cells, 0, width, axis=dim)
        tail = lax.slice_in_dim(cells, cells.shape[dim] - width, cells.shape[dim], axis=dim)
        cells = jnp.concatenate(
            [
                lax.ppermute(tail, axis, [(i, (i + 1) % count) for i in range(ends)]),
                cells,
                lax.ppermute(head, axis, [((i + 1) % count, i) for i in range(ends)]),
            ],
            axis=dim,
        )
    return cells


def standardize_rows(columns_in):
    values = columns_in.astype(jnp.float32)
    average = jnp.mean(values, 0, keepdims=True)
    centred = values - average
    spread = jnp.mean(centred * centred, 0, keepdims=True)
    inverse_deviation = lax.rsqrt(spread + 1e-05)
    return (centred * inverse_deviation, inverse_deviation)


def depthwise(padded, kernel):
    channels = padded.shape[0]
    result = lax.conv_general_dilated(
        padded[None],
        kernel,
        (1,),
        "VALID",
        dimension_numbers=("NCH", "OIH", "NCH"),
        feature_group_count=channels,
        precision=lax.Precision.HIGHEST,
    )
    return result[0]


def gather_by_exchange(block, axis):
    count = lax.axis_size(axis)
    copies = jnp.broadcast_to(block[None], (count,) + block.shape)
    return lax.all_to_all(copies, axis, 0, 0, tiled=False)


def bf16_pieces(values, pieces):
    parts = []
    rest = values
    for _ in range(pieces):
        part = rest.astype(jnp.bfloat16)
        parts.append(part)
        rest = rest - part.astype(jnp.float32)
    return parts


def gather_by_shifts(block, axis):
    count = lax.axis_size(axis)
    position = lax.axis_index(axis)
    pieces = [block]
    for shift in range(1, count):
        pieces.append(
            lax.ppermute(block, axis, [(i, (i - shift) % count) for i in range(count)])
        )
    return jnp.roll(jnp.stack(pieces, 0), position, axis=0)


def reduce_by_shifts(blocks, rider, axis):
    count = lax.axis_size(axis)
    position = lax.axis_index(axis)
    total = lax.dynamic_index_in_dim(blocks, position, 0, keepdims=False).astype(jnp.float32)
    riders = rider.astype(jnp.float32)
    rows = blocks.shape[1]
    for shift in range(1, count):
        outgoing = lax.dynamic_index_in_dim(blocks, (position + shift) % count, 0, keepdims=False)
        outgoing = jnp.concatenate([outgoing, rider], 0)
        arrived = lax.ppermute(outgoing, axis, [(i, (i + shift) % count) for i in range(count)])
        total = total + arrived[:rows].astype(jnp.float32)
        riders = riders + arrived[rows:].astype(jnp.float32)
    return total, riders


def shifted_sum(padded, taps, span):
    total = taps[0][:, None] * padded[:, 0:span]
    for k in range(1, taps.shape[0]):
        total = total + taps[k][:, None] * padded[:, k : k + span]
    return total


def shards(signal, input_norm_gain, value_weight, gate_weight, depth_taps, cotangent):
    local_cols, frames = signal.shape
    groups = lax.axis_size("ch")
    blocks = lax.axis_size("seq")
    channel_position = lax.axis_index("ch")
    reach = depth_taps.shape[0] // 2
    gain_rows = jnp.stack(bf16_pieces(input_norm_gain, 3), 0)
    gain_rows = jnp.pad(gain_rows, ((0, 13), (0, frames - local_cols)))
    arrived = lax.all_gather(jnp.concatenate([signal, gain_rows], 0), "ch", axis=0)
    complete_signal = arrived[:, :local_cols].reshape(groups * local_cols, frames)
    gain_parts = arrived[:, local_cols : local_cols + 3, :local_cols].astype(jnp.float32)
    complete_gain = ((gain_parts[:, 0] + gain_parts[:, 1]) + gain_parts[:, 2]).reshape(-1)
    centered_unit, inverse_deviation = standardize_rows(complete_signal)
    normalized_signal = (centered_unit * complete_gain[:, None]).astype(jnp.bfloat16)
    centered_unit_rows = lax.dynamic_slice_in_dim(
        centered_unit, channel_position * local_cols, local_cols, 0
    )
    stacked = jnp.concatenate([value_weight, gate_weight], 1)
    gathered = gather_by_exchange(stacked, "seq").reshape(-1, stacked.shape[1])
    mixed = lax.dot_general(
        gathered, normalized_signal, (((0,), (0,)), ((), ())), preferred_element_type=jnp.float32
    )
    value = mixed[:local_cols]
    gate = mixed[local_cols:]
    sig_gate = jax.nn.sigmoid(gate)
    glued = (value * sig_gate).astype(jnp.bfloat16)
    glued_pad = extended(glued, (("seq", 1),), reach).astype(jnp.float32)
    span = glued.shape[1]
    taps_count = depth_taps.shape[0]
    pre = shifted_sum(glued_pad, depth_taps, span)
    sig_pre = jax.nn.sigmoid(pre)
    output = (pre * sig_pre).astype(jnp.bfloat16)
    grad_pre = (cotangent.astype(jnp.float32) * sig_pre * (1.0 + pre * (1.0 - sig_pre))).astype(
        jnp.bfloat16
    )
    grad_pre_f = grad_pre.astype(jnp.float32)
    grad_pad = extended(grad_pre, (("seq", 1),), reach).astype(jnp.float32)
    grad_glued = shifted_sum(grad_pad, depth_taps[::-1], span)
    tap_partial = jnp.stack(
        [jnp.sum(glued_pad[:, k : k + span] * grad_pre_f, 1) for k in range(taps_count)], 0
    )
    grad_v = (grad_glued * sig_gate).astype(jnp.bfloat16)
    grad_g = (grad_glued * value * sig_gate * (1.0 - sig_gate)).astype(jnp.bfloat16)
    grad_both = jnp.concatenate([grad_v, grad_g], 0)
    weight_partial = lax.dot_general(
        normalized_signal,
        grad_both,
        (((1,), (1,)), ((), ())),
        preferred_element_type=jnp.float32,
    )
    normed_term = jnp.dot(gathered, grad_both, preferred_element_type=jnp.float32).astype(
        jnp.bfloat16
    )
    width = weight_partial.shape[1]
    rows = value_weight.shape[0]
    taps_rows = depth_taps.shape[0]
    taps_flat = jnp.pad(tap_partial, ((0, 1), (0, 0))).reshape(blocks, -1)
    piece = taps_flat.shape[1]
    taps_row = jnp.concatenate(bf16_pieces(taps_flat, 3), 1)
    taps_row = jnp.pad(taps_row, ((0, 0), (0, width - taps_row.shape[1])))
    outgoing = jnp.concatenate(
        [weight_partial.astype(jnp.bfloat16).reshape(blocks, rows, width), taps_row[:, None]], 1
    )
    summed = jnp.sum(lax.all_to_all(outgoing, "seq", 0, 0, tiled=False).astype(jnp.float32), 0)
    weight_sums = summed[:rows]
    taps_summed = (summed[rows, :piece] + summed[rows, piece : 2 * piece]) + summed[
        rows, 2 * piece : 3 * piece
    ]
    grad_value = weight_sums[:, :local_cols]
    grad_gate = weight_sums[:, local_cols:]
    normed_f = normed_term.astype(jnp.float32)
    weighted = normed_f * complete_gain[:, None]
    own_moments = jnp.stack([jnp.sum(weighted, 0), jnp.sum(weighted * centered_unit, 0)], 0)
    moment_rows = jnp.concatenate(bf16_pieces(own_moments, 3), 0)
    half = frames // 2
    split = frames - frames // 4
    moment_rows = moment_rows.reshape(-1, frames - split)
    used_rows = moment_rows.shape[0]
    moment_rows = jnp.pad(moment_rows, ((0, 32 - used_rows), (0, 0)))
    early_part = lax.psum_scatter(
        normed_term[:, :split], "ch", scatter_dimension=0, tiled=True
    ).astype(jnp.float32)
    late_part, moment_total = reduce_by_shifts(
        normed_term[:, split:].reshape(groups, local_cols, frames - split), moment_rows, "ch"
    )
    normalized_gradient = jnp.concatenate([early_part, late_part], 1)
    moment_total = moment_total[:used_rows].reshape(6, frames)
    scaled_signal = normalized_gradient * input_norm_gain[:, None]
    moments = ((moment_total[0:2] + moment_total[2:4]) + moment_total[4:6]) * (
        1.0 / complete_signal.shape[0]
    )
    signal_gradient = (
        inverse_deviation
        * (scaled_signal - moments[0:1] - centered_unit_rows * moments[1:2])
    ).astype(jnp.bfloat16)
    gain_portion = jnp.sum(normalized_gradient * centered_unit_rows, 1)
    last = jnp.concatenate([taps_summed, gain_portion], 0)
    finished = gather_by_exchange(last, "seq")
    grad_taps = finished[:, :piece].reshape(-1)[: taps_rows * local_cols].reshape(
        taps_rows, local_cols
    )
    gain_gradient = jnp.sum(finished[:, piece:], 0)
    return (output, signal_gradient, grad_value, grad_gate, grad_taps, gain_gradient)


def solution(mesh):
    placed = (
        P("ch", "seq"),
        P("ch"),
        P("seq", "ch"),
        P("seq", "ch"),
        P(None, "ch"),
        P("ch", "seq"),
    )
    return jax.shard_map(
        shards,
        mesh=mesh,
        in_specs=placed,
        out_specs=(
            P("ch", "seq"),
            P("ch", "seq"),
            P("seq", "ch"),
            P("seq", "ch"),
            P(None, "ch"),
            P("ch"),
        ),
        check_vma=False,
    )
```

```python
import jax
import jax.numpy as jnp
from jax import lax
from jax.sharding import PartitionSpec as P


def extended(cells, sides, width):
    for axis, dim in sides:
        count = lax.axis_size(axis)
        ends = count - 1
        head = lax.slice_in_dim(cells, 0, width, axis=dim)
        tail = lax.slice_in_dim(cells, cells.shape[dim] - width, cells.shape[dim], axis=dim)
        cells = jnp.concatenate(
            [
                lax.ppermute(tail, axis, [(i, (i + 1) % count) for i in range(ends)]),
                cells,
                lax.ppermute(head, axis, [((i + 1) % count, i) for i in range(ends)]),
            ],
            axis=dim,
        )
    return cells


def standardize_rows(columns_in):
    values = columns_in.astype(jnp.float32)
    average = jnp.mean(values, 0, keepdims=True)
    centred = values - average
    spread = jnp.mean(centred * centred, 0, keepdims=True)
    inverse_deviation = lax.rsqrt(spread + 1e-05)
    return (centred * inverse_deviation, inverse_deviation)


def depthwise(padded, kernel):
    channels = padded.shape[0]
    result = lax.conv_general_dilated(
        padded[None],
        kernel,
        (1,),
        "VALID",
        dimension_numbers=("NCH", "OIH", "NCH"),
        feature_group_count=channels,
        precision=lax.Precision.HIGHEST,
    )
    return result[0]


def gather_by_exchange(block, axis):
    count = lax.axis_size(axis)
    copies = jnp.broadcast_to(block[None], (count,) + block.shape)
    return lax.all_to_all(copies, axis, 0, 0, tiled=False)


def bf16_pieces(values, pieces):
    parts = []
    rest = values
    for _ in range(pieces):
        part = rest.astype(jnp.bfloat16)
        parts.append(part)
        rest = rest - part.astype(jnp.float32)
    return parts


def gather_by_shifts(block, axis):
    count = lax.axis_size(axis)
    position = lax.axis_index(axis)
    pieces = [block]
    for shift in range(1, count):
        pieces.append(
            lax.ppermute(block, axis, [(i, (i - shift) % count) for i in range(count)])
        )
    return jnp.roll(jnp.stack(pieces, 0), position, axis=0)


def reduce_by_shifts(blocks, rider, axis):
    count = lax.axis_size(axis)
    position = lax.axis_index(axis)
    total = lax.dynamic_index_in_dim(blocks, position, 0, keepdims=False).astype(jnp.float32)
    riders = rider.astype(jnp.float32)
    rows = blocks.shape[1]
    for shift in range(1, count):
        outgoing = lax.dynamic_index_in_dim(blocks, (position + shift) % count, 0, keepdims=False)
        outgoing = jnp.concatenate([outgoing, rider], 0)
        arrived = lax.ppermute(outgoing, axis, [(i, (i + shift) % count) for i in range(count)])
        total = total + arrived[:rows].astype(jnp.float32)
        riders = riders + arrived[rows:].astype(jnp.float32)
    return total, riders


def shifted_sum(padded, taps, span):
    total = taps[0][:, None] * padded[:, 0:span]
    for k in range(1, taps.shape[0]):
        total = total + taps[k][:, None] * padded[:, k : k + span]
    return total


def shards(signal, input_norm_gain, value_weight, gate_weight, depth_taps, cotangent):
    local_cols, frames = signal.shape
    groups = lax.axis_size("ch")
    blocks = lax.axis_size("seq")
    channel_position = lax.axis_index("ch")
    reach = depth_taps.shape[0] // 2
    gain_rows = jnp.stack(bf16_pieces(input_norm_gain, 3), 0)
    cut = frames - frames // 4
    gain_rows = jnp.pad(gain_rows, ((0, 13), (0, cut - local_cols)))
    arrived = lax.all_gather(jnp.concatenate([signal[:, :cut], gain_rows], 0), "ch", axis=0)
    arrived_late = gather_by_shifts(signal[:, cut:], "ch")
    complete_signal = jnp.concatenate([arrived[:, :local_cols], arrived_late], 2).reshape(
        groups * local_cols, frames
    )
    gain_parts = arrived[:, local_cols : local_cols + 3, :local_cols].astype(jnp.float32)
    complete_gain = ((gain_parts[:, 0] + gain_parts[:, 1]) + gain_parts[:, 2]).reshape(-1)
    centered_unit, inverse_deviation = standardize_rows(complete_signal)
    normalized_signal = (centered_unit * complete_gain[:, None]).astype(jnp.bfloat16)
    centered_unit_rows = lax.dynamic_slice_in_dim(
        centered_unit, channel_position * local_cols, local_cols, 0
    )
    stacked = jnp.concatenate([value_weight, gate_weight], 1)
    gathered = gather_by_exchange(stacked, "seq").reshape(-1, stacked.shape[1])
    mixed = lax.dot_general(
        gathered, normalized_signal, (((0,), (0,)), ((), ())), preferred_element_type=jnp.float32
    )
    value = mixed[:local_cols]
    gate = mixed[local_cols:]
    sig_gate = jax.nn.sigmoid(gate)
    glued = (value * sig_gate).astype(jnp.bfloat16)
    glued_pad = extended(glued, (("seq", 1),), reach).astype(jnp.float32)
    span = glued.shape[1]
    taps_count = depth_taps.shape[0]
    pre = shifted_sum(glued_pad, depth_taps, span)
    sig_pre = jax.nn.sigmoid(pre)
    output = (pre * sig_pre).astype(jnp.bfloat16)
    grad_pre = (cotangent.astype(jnp.float32) * sig_pre * (1.0 + pre * (1.0 - sig_pre))).astype(
        jnp.bfloat16
    )
    grad_pre_f = grad_pre.astype(jnp.float32)
    grad_pad = extended(grad_pre, (("seq", 1),), reach).astype(jnp.float32)
    grad_glued = shifted_sum(grad_pad, depth_taps[::-1], span)
    tap_partial = jnp.stack(
        [jnp.sum(glued_pad[:, k : k + span] * grad_pre_f, 1) for k in range(taps_count)], 0
    )
    grad_v = (grad_glued * sig_gate).astype(jnp.bfloat16)
    grad_g = (grad_glued * value * sig_gate * (1.0 - sig_gate)).astype(jnp.bfloat16)
    grad_both = jnp.concatenate([grad_v, grad_g], 0)
    weight_partial = lax.dot_general(
        normalized_signal,
        grad_both,
        (((1,), (1,)), ((), ())),
        preferred_element_type=jnp.float32,
    )
    normed_term = jnp.dot(gathered, grad_both, preferred_element_type=jnp.float32).astype(
        jnp.bfloat16
    )
    width = weight_partial.shape[1]
    rows = value_weight.shape[0]
    taps_rows = depth_taps.shape[0]
    taps_flat = jnp.pad(tap_partial, ((0, 1), (0, 0))).reshape(blocks, -1)
    piece = taps_flat.shape[1]
    taps_row = jnp.concatenate(bf16_pieces(taps_flat, 3), 1)
    taps_row = jnp.pad(taps_row, ((0, 0), (0, width - taps_row.shape[1])))
    outgoing = jnp.concatenate(
        [weight_partial.astype(jnp.bfloat16).reshape(blocks, rows, width), taps_row[:, None]], 1
    )
    summed = jnp.sum(lax.all_to_all(outgoing, "seq", 0, 0, tiled=False).astype(jnp.float32), 0)
    weight_sums = summed[:rows]
    taps_summed = (summed[rows, :piece] + summed[rows, piece : 2 * piece]) + summed[
        rows, 2 * piece : 3 * piece
    ]
    grad_value = weight_sums[:, :local_cols]
    grad_gate = weight_sums[:, local_cols:]
    normed_f = normed_term.astype(jnp.float32)
    weighted = normed_f * complete_gain[:, None]
    own_moments = jnp.stack([jnp.sum(weighted, 0), jnp.sum(weighted * centered_unit, 0)], 0)
    moment_rows = jnp.concatenate(bf16_pieces(own_moments, 3), 0)
    half = frames // 2
    split = frames - frames // 4
    moment_rows = moment_rows.reshape(-1, frames - split)
    used_rows = moment_rows.shape[0]
    moment_rows = jnp.pad(moment_rows, ((0, 32 - used_rows), (0, 0)))
    early_part = lax.psum_scatter(
        normed_term[:, :split], "ch", scatter_dimension=0, tiled=True
    ).astype(jnp.float32)
    late_part, moment_total = reduce_by_shifts(
        normed_term[:, split:].reshape(groups, local_cols, frames - split), moment_rows, "ch"
    )
    normalized_gradient = jnp.concatenate([early_part, late_part], 1)
    moment_total = moment_total[:used_rows].reshape(6, frames)
    scaled_signal = normalized_gradient * input_norm_gain[:, None]
    moments = ((moment_total[0:2] + moment_total[2:4]) + moment_total[4:6]) * (
        1.0 / complete_signal.shape[0]
    )
    signal_gradient = (
        inverse_deviation
        * (scaled_signal - moments[0:1] - centered_unit_rows * moments[1:2])
    ).astype(jnp.bfloat16)
    gain_portion = jnp.sum(normalized_gradient * centered_unit_rows, 1)
    last = jnp.concatenate([taps_summed, gain_portion], 0)
    finished = gather_by_exchange(last, "seq")
    grad_taps = finished[:, :piece].reshape(-1)[: taps_rows * local_cols].reshape(
        taps_rows, local_cols
    )
    gain_gradient = jnp.sum(finished[:, piece:], 0)
    return (output, signal_gradient, grad_value, grad_gate, grad_taps, gain_gradient)


def solution(mesh):
    placed = (
        P("ch", "seq"),
        P("ch"),
        P("seq", "ch"),
        P("seq", "ch"),
        P(None, "ch"),
        P("ch", "seq"),
    )
    return jax.shard_map(
        shards,
        mesh=mesh,
        in_specs=placed,
        out_specs=(
            P("ch", "seq"),
            P("ch", "seq"),
            P("seq", "ch"),
            P("seq", "ch"),
            P(None, "ch"),
            P("ch"),
        ),
        check_vma=False,
    )
```

```python
import jax
import jax.numpy as jnp
from jax import lax
from jax.sharding import PartitionSpec as P


def extended(cells, sides, width):
    for axis, dim in sides:
        count = lax.axis_size(axis)
        ends = count - 1
        head = lax.slice_in_dim(cells, 0, width, axis=dim)
        tail = lax.slice_in_dim(cells, cells.shape[dim] - width, cells.shape[dim], axis=dim)
        cells = jnp.concatenate(
            [
                lax.ppermute(tail, axis, [(i, (i + 1) % count) for i in range(ends)]),
                cells,
                lax.ppermute(head, axis, [((i + 1) % count, i) for i in range(ends)]),
            ],
            axis=dim,
        )
    return cells


def standardize_rows(columns_in):
    values = columns_in.astype(jnp.float32)
    average = jnp.mean(values, 0, keepdims=True)
    centred = values - average
    spread = jnp.mean(centred * centred, 0, keepdims=True)
    inverse_deviation = lax.rsqrt(spread + 1e-05)
    return (centred * inverse_deviation, inverse_deviation)


def depthwise(padded, kernel):
    channels = padded.shape[0]
    result = lax.conv_general_dilated(
        padded[None],
        kernel,
        (1,),
        "VALID",
        dimension_numbers=("NCH", "OIH", "NCH"),
        feature_group_count=channels,
        precision=lax.Precision.HIGHEST,
    )
    return result[0]


def gather_by_exchange(block, axis):
    count = lax.axis_size(axis)
    copies = jnp.broadcast_to(block[None], (count,) + block.shape)
    return lax.all_to_all(copies, axis, 0, 0, tiled=False)


def bf16_pieces(values, pieces):
    parts = []
    rest = values
    for _ in range(pieces):
        part = rest.astype(jnp.bfloat16)
        parts.append(part)
        rest = rest - part.astype(jnp.float32)
    return parts


def gather_by_shifts(block, axis):
    count = lax.axis_size(axis)
    position = lax.axis_index(axis)
    pieces = [block]
    for shift in range(1, count):
        pieces.append(
            lax.ppermute(block, axis, [(i, (i - shift) % count) for i in range(count)])
        )
    return jnp.roll(jnp.stack(pieces, 0), position, axis=0)


def reduce_by_shifts(blocks, rider, axis):
    count = lax.axis_size(axis)
    position = lax.axis_index(axis)
    total = lax.dynamic_index_in_dim(blocks, position, 0, keepdims=False).astype(jnp.float32)
    riders = rider.astype(jnp.float32)
    rows = blocks.shape[1]
    for shift in range(1, count):
        outgoing = lax.dynamic_index_in_dim(blocks, (position + shift) % count, 0, keepdims=False)
        outgoing = jnp.concatenate([outgoing, rider], 0)
        arrived = lax.ppermute(outgoing, axis, [(i, (i + shift) % count) for i in range(count)])
        total = total + arrived[:rows].astype(jnp.float32)
        riders = riders + arrived[rows:].astype(jnp.float32)
    return total, riders


def shifted_sum(padded, taps, span):
    total = taps[0][:, None] * padded[:, 0:span]
    for k in range(1, taps.shape[0]):
        total = total + taps[k][:, None] * padded[:, k : k + span]
    return total


def shards(signal, input_norm_gain, value_weight, gate_weight, depth_taps, cotangent):
    local_cols, frames = signal.shape
    groups = lax.axis_size("ch")
    blocks = lax.axis_size("seq")
    channel_position = lax.axis_index("ch")
    reach = depth_taps.shape[0] // 2
    gain_rows = jnp.stack(bf16_pieces(input_norm_gain, 3), 0)
    gain_rows = jnp.pad(gain_rows, ((0, 13), (0, frames - local_cols)))
    arrived = lax.all_gather(jnp.concatenate([signal, gain_rows], 0), "ch", axis=0)
    complete_signal = arrived[:, :local_cols].reshape(groups * local_cols, frames)
    gain_parts = arrived[:, local_cols : local_cols + 3, :local_cols].astype(jnp.float32)
    complete_gain = ((gain_parts[:, 0] + gain_parts[:, 1]) + gain_parts[:, 2]).reshape(-1)
    centered_unit, inverse_deviation = standardize_rows(complete_signal)
    normalized_signal = (centered_unit * complete_gain[:, None]).astype(jnp.bfloat16)
    centered_unit_rows = lax.dynamic_slice_in_dim(
        centered_unit, channel_position * local_cols, local_cols, 0
    )
    stacked = jnp.concatenate([value_weight, gate_weight], 1)
    gathered = gather_by_exchange(stacked, "seq").reshape(-1, stacked.shape[1])
    mixed = lax.dot_general(
        gathered, normalized_signal, (((0,), (0,)), ((), ())), preferred_element_type=jnp.float32
    )
    value = mixed[:local_cols]
    gate = mixed[local_cols:]
    sig_gate = jax.nn.sigmoid(gate)
    glued = (value * sig_gate).astype(jnp.bfloat16)
    glued_pad = extended(glued, (("seq", 1),), reach).astype(jnp.float32)
    span = glued.shape[1]
    taps_count = depth_taps.shape[0]
    pre = shifted_sum(glued_pad, depth_taps, span)
    sig_pre = jax.nn.sigmoid(pre)
    output = (pre * sig_pre).astype(jnp.bfloat16)
    grad_pre = (cotangent.astype(jnp.float32) * sig_pre * (1.0 + pre * (1.0 - sig_pre))).astype(
        jnp.bfloat16
    )
    grad_pre_f = grad_pre.astype(jnp.float32)
    grad_pad = extended(grad_pre, (("seq", 1),), reach).astype(jnp.float32)
    grad_glued = shifted_sum(grad_pad, depth_taps[::-1], span)
    windows = jnp.stack([glued_pad[:, k : k + span] for k in range(taps_count)], 0)
    tap_partial = jnp.sum(windows * grad_pre_f[None], 2)
    grad_v = (grad_glued * sig_gate).astype(jnp.bfloat16)
    grad_g = (grad_glued * value * sig_gate * (1.0 - sig_gate)).astype(jnp.bfloat16)
    grad_both = jnp.concatenate([grad_v, grad_g], 0)
    weight_partial = lax.dot_general(
        normalized_signal,
        grad_both,
        (((1,), (1,)), ((), ())),
        preferred_element_type=jnp.float32,
    )
    normed_term = jnp.dot(gathered, grad_both, preferred_element_type=jnp.float32).astype(
        jnp.bfloat16
    )
    width = weight_partial.shape[1]
    rows = value_weight.shape[0]
    taps_rows = depth_taps.shape[0]
    taps_flat = jnp.pad(tap_partial, ((0, 1), (0, 0))).reshape(blocks, -1)
    piece = taps_flat.shape[1]
    taps_row = jnp.concatenate(bf16_pieces(taps_flat, 3), 1)
    taps_row = jnp.pad(taps_row, ((0, 0), (0, width - taps_row.shape[1])))
    outgoing = jnp.concatenate(
        [weight_partial.astype(jnp.bfloat16).reshape(blocks, rows, width), taps_row[:, None]], 1
    )
    summed = jnp.sum(lax.all_to_all(outgoing, "seq", 0, 0, tiled=False).astype(jnp.float32), 0)
    weight_sums = summed[:rows]
    taps_summed = (summed[rows, :piece] + summed[rows, piece : 2 * piece]) + summed[
        rows, 2 * piece : 3 * piece
    ]
    grad_value = weight_sums[:, :local_cols]
    grad_gate = weight_sums[:, local_cols:]
    normed_f = normed_term.astype(jnp.float32)
    weighted = normed_f * complete_gain[:, None]
    own_moments = jnp.stack([jnp.sum(weighted, 0), jnp.sum(weighted * centered_unit, 0)], 0)
    moment_rows = jnp.concatenate(bf16_pieces(own_moments, 3), 0)
    half = frames // 2
    split = frames - frames // 4
    moment_rows = moment_rows.reshape(-1, frames - split)
    used_rows = moment_rows.shape[0]
    moment_rows = jnp.pad(moment_rows, ((0, 32 - used_rows), (0, 0)))
    early_part = lax.psum_scatter(
        normed_term[:, :split], "ch", scatter_dimension=0, tiled=True
    ).astype(jnp.float32)
    late_part, moment_total = reduce_by_shifts(
        normed_term[:, split:].reshape(groups, local_cols, frames - split), moment_rows, "ch"
    )
    normalized_gradient = jnp.concatenate([early_part, late_part], 1)
    moment_total = moment_total[:used_rows].reshape(6, frames)
    scaled_signal = normalized_gradient * input_norm_gain[:, None]
    moments = ((moment_total[0:2] + moment_total[2:4]) + moment_total[4:6]) * (
        1.0 / complete_signal.shape[0]
    )
    signal_gradient = (
        inverse_deviation
        * (scaled_signal - moments[0:1] - centered_unit_rows * moments[1:2])
    ).astype(jnp.bfloat16)
    gain_portion = jnp.sum(normalized_gradient * centered_unit_rows, 1)
    last = jnp.concatenate([taps_summed, gain_portion], 0)
    finished = gather_by_exchange(last, "seq")
    grad_taps = finished[:, :piece].reshape(-1)[: taps_rows * local_cols].reshape(
        taps_rows, local_cols
    )
    gain_gradient = jnp.sum(finished[:, piece:], 0)
    return (output, signal_gradient, grad_value, grad_gate, grad_taps, gain_gradient)


def solution(mesh):
    placed = (
        P("ch", "seq"),
        P("ch"),
        P("seq", "ch"),
        P("seq", "ch"),
        P(None, "ch"),
        P("ch", "seq"),
    )
    return jax.shard_map(
        shards,
        mesh=mesh,
        in_specs=placed,
        out_specs=(
            P("ch", "seq"),
            P("ch", "seq"),
            P("seq", "ch"),
            P("seq", "ch"),
            P(None, "ch"),
            P("ch"),
        ),
        check_vma=False,
    )
```

```python
import jax
import jax.numpy as jnp
from jax import lax
from jax.sharding import PartitionSpec as P


def extended(cells, sides, width):
    for axis, dim in sides:
        count = lax.axis_size(axis)
        ends = count - 1
        head = lax.slice_in_dim(cells, 0, width, axis=dim)
        tail = lax.slice_in_dim(cells, cells.shape[dim] - width, cells.shape[dim], axis=dim)
        cells = jnp.concatenate(
            [
                lax.ppermute(tail, axis, [(i, (i + 1) % count) for i in range(ends)]),
                cells,
                lax.ppermute(head, axis, [((i + 1) % count, i) for i in range(ends)]),
            ],
            axis=dim,
        )
    return cells


def standardize_rows(columns_in):
    values = columns_in.astype(jnp.float32)
    average = jnp.mean(values, 0, keepdims=True)
    centred = values - average
    spread = jnp.mean(centred * centred, 0, keepdims=True)
    inverse_deviation = lax.rsqrt(spread + 1e-05)
    return (centred * inverse_deviation, inverse_deviation)


def depthwise(padded, kernel):
    channels = padded.shape[0]
    result = lax.conv_general_dilated(
        padded[None],
        kernel,
        (1,),
        "VALID",
        dimension_numbers=("NCH", "OIH", "NCH"),
        feature_group_count=channels,
        precision=lax.Precision.HIGHEST,
    )
    return result[0]


def gather_by_exchange(block, axis):
    count = lax.axis_size(axis)
    copies = jnp.broadcast_to(block[None], (count,) + block.shape)
    return lax.all_to_all(copies, axis, 0, 0, tiled=False)


def bf16_pieces(values, pieces):
    parts = []
    rest = values
    for _ in range(pieces):
        part = rest.astype(jnp.bfloat16)
        parts.append(part)
        rest = rest - part.astype(jnp.float32)
    return parts


def gather_by_shifts(block, axis):
    count = lax.axis_size(axis)
    position = lax.axis_index(axis)
    pieces = [block]
    for shift in range(1, count):
        pieces.append(
            lax.ppermute(block, axis, [(i, (i - shift) % count) for i in range(count)])
        )
    return jnp.roll(jnp.stack(pieces, 0), position, axis=0)


def reduce_by_shifts(blocks, rider, axis):
    count = lax.axis_size(axis)
    position = lax.axis_index(axis)
    total = lax.dynamic_index_in_dim(blocks, position, 0, keepdims=False).astype(jnp.float32)
    riders = rider.astype(jnp.float32)
    rows = blocks.shape[1]
    for shift in range(1, count):
        outgoing = lax.dynamic_index_in_dim(blocks, (position + shift) % count, 0, keepdims=False)
        outgoing = jnp.concatenate([outgoing, rider], 0)
        arrived = lax.ppermute(outgoing, axis, [(i, (i + shift) % count) for i in range(count)])
        total = total + arrived[:rows].astype(jnp.float32)
        riders = riders + arrived[rows:].astype(jnp.float32)
    return total, riders


def shifted_sum(padded, taps, span):
    total = taps[0][:, None] * padded[:, 0:span]
    for k in range(1, taps.shape[0]):
        total = total + taps[k][:, None] * padded[:, k : k + span]
    return total


def shards(signal, input_norm_gain, value_weight, gate_weight, depth_taps, cotangent):
    local_cols, frames = signal.shape
    groups = lax.axis_size("ch")
    blocks = lax.axis_size("seq")
    channel_position = lax.axis_index("ch")
    reach = depth_taps.shape[0] // 2
    gain_rows = jnp.stack(bf16_pieces(input_norm_gain, 3), 0)
    gain_rows = jnp.pad(gain_rows, ((0, 13), (0, frames - local_cols)))
    arrived = lax.all_gather(jnp.concatenate([signal, gain_rows], 0), "ch", axis=0)
    complete_signal = arrived[:, :local_cols].reshape(groups * local_cols, frames)
    gain_parts = arrived[:, local_cols : local_cols + 3, :local_cols].astype(jnp.float32)
    complete_gain = ((gain_parts[:, 0] + gain_parts[:, 1]) + gain_parts[:, 2]).reshape(-1)
    centered_unit, inverse_deviation = standardize_rows(complete_signal)
    normalized_signal = (centered_unit * complete_gain[:, None]).astype(jnp.bfloat16)
    centered_unit_rows = lax.dynamic_slice_in_dim(
        centered_unit, channel_position * local_cols, local_cols, 0
    )
    stacked = jnp.concatenate([value_weight, gate_weight], 1)
    gathered = gather_by_exchange(stacked, "seq").reshape(-1, stacked.shape[1])
    mixed = lax.dot_general(
        gathered, normalized_signal, (((0,), (0,)), ((), ())), preferred_element_type=jnp.float32
    )
    value = mixed[:local_cols]
    gate = mixed[local_cols:]
    sig_gate = jax.nn.sigmoid(gate)
    glued = (value * sig_gate).astype(jnp.bfloat16)
    glued_pad = extended(glued, (("seq", 1),), reach).astype(jnp.float32)
    span = glued.shape[1]
    taps_count = depth_taps.shape[0]
    pre = shifted_sum(glued_pad, depth_taps, span)
    sig_pre = jax.nn.sigmoid(pre)
    output = (pre * sig_pre).astype(jnp.bfloat16)
    grad_pre = (cotangent.astype(jnp.float32) * sig_pre * (1.0 + pre * (1.0 - sig_pre))).astype(
        jnp.bfloat16
    )
    grad_pre_f = grad_pre.astype(jnp.float32)
    grad_pad = extended(grad_pre, (("seq", 1),), reach).astype(jnp.float32)
    grad_glued = shifted_sum(grad_pad, depth_taps[::-1], span)
    tap_partial = jnp.stack(
        [jnp.sum(glued_pad[:, k : k + span] * grad_pre_f, 1) for k in range(taps_count)], 0
    )
    grad_v = (grad_glued * sig_gate).astype(jnp.bfloat16)
    grad_g = (grad_glued * value * sig_gate * (1.0 - sig_gate)).astype(jnp.bfloat16)
    grad_both = jnp.concatenate([grad_v, grad_g], 0)
    weight_partial = lax.dot_general(
        normalized_signal,
        grad_both,
        (((1,), (1,)), ((), ())),
        preferred_element_type=jnp.float32,
    )
    normed_term = jnp.dot(gathered, grad_both, preferred_element_type=jnp.float32).astype(
        jnp.bfloat16
    )
    width = weight_partial.shape[1]
    rows = value_weight.shape[0]
    taps_rows = depth_taps.shape[0]
    taps_flat = jnp.pad(tap_partial, ((0, 1), (0, 0))).reshape(blocks, -1)
    piece = taps_flat.shape[1]
    taps_row = jnp.concatenate(bf16_pieces(taps_flat, 3), 1)
    taps_row = jnp.pad(taps_row, ((0, 0), (0, width - taps_row.shape[1])))
    outgoing = jnp.concatenate(
        [weight_partial.astype(jnp.bfloat16).reshape(blocks, rows, width), taps_row[:, None]], 1
    )
    summed = jnp.sum(lax.all_to_all(outgoing, "seq", 0, 0, tiled=False).astype(jnp.float32), 0)
    weight_sums = summed[:rows]
    taps_summed = (summed[rows, :piece] + summed[rows, piece : 2 * piece]) + summed[
        rows, 2 * piece : 3 * piece
    ]
    grad_value = weight_sums[:, :local_cols]
    grad_gate = weight_sums[:, local_cols:]
    normed_f = normed_term.astype(jnp.float32)
    weighted = normed_f * complete_gain[:, None]
    own_moments = jnp.stack([jnp.sum(weighted, 0), jnp.sum(weighted * centered_unit, 0)], 0)
    normalized_gradient = lax.psum_scatter(
        normed_term, "ch", scatter_dimension=0, tiled=True
    ).astype(jnp.float32)
    scaled_signal = normalized_gradient * input_norm_gain[:, None]
    moments = lax.psum(own_moments, "ch") * (1.0 / complete_signal.shape[0])
    signal_gradient = (
        inverse_deviation
        * (scaled_signal - moments[0:1] - centered_unit_rows * moments[1:2])
    ).astype(jnp.bfloat16)
    gain_portion = jnp.sum(normalized_gradient * centered_unit_rows, 1)
    last = jnp.concatenate([taps_summed, gain_portion], 0)
    finished = gather_by_exchange(last, "seq")
    grad_taps = finished[:, :piece].reshape(-1)[: taps_rows * local_cols].reshape(
        taps_rows, local_cols
    )
    gain_gradient = jnp.sum(finished[:, piece:], 0)
    return (output, signal_gradient, grad_value, grad_gate, grad_taps, gain_gradient)


def solution(mesh):
    placed = (
        P("ch", "seq"),
        P("ch"),
        P("seq", "ch"),
        P("seq", "ch"),
        P(None, "ch"),
        P("ch", "seq"),
    )
    return jax.shard_map(
        shards,
        mesh=mesh,
        in_specs=placed,
        out_specs=(
            P("ch", "seq"),
            P("ch", "seq"),
            P("seq", "ch"),
            P("seq", "ch"),
            P(None, "ch"),
            P("ch"),
        ),
        check_vma=False,
    )
```

```python
import jax
import jax.numpy as jnp
from jax import lax
from jax.sharding import PartitionSpec as P


def extended(cells, sides, width):
    for axis, dim in sides:
        count = lax.axis_size(axis)
        ends = count - 1
        head = lax.slice_in_dim(cells, 0, width, axis=dim)
        tail = lax.slice_in_dim(cells, cells.shape[dim] - width, cells.shape[dim], axis=dim)
        cells = jnp.concatenate(
            [
                lax.ppermute(tail, axis, [(i, (i + 1) % count) for i in range(ends)]),
                cells,
                lax.ppermute(head, axis, [((i + 1) % count, i) for i in range(ends)]),
            ],
            axis=dim,
        )
    return cells


def standardize_rows(columns_in):
    values = columns_in.astype(jnp.float32)
    average = jnp.mean(values, 0, keepdims=True)
    centred = values - average
    spread = jnp.mean(centred * centred, 0, keepdims=True)
    inverse_deviation = lax.rsqrt(spread + 1e-05)
    return (centred * inverse_deviation, inverse_deviation)


def depthwise(padded, kernel):
    channels = padded.shape[0]
    result = lax.conv_general_dilated(
        padded[None],
        kernel,
        (1,),
        "VALID",
        dimension_numbers=("NCH", "OIH", "NCH"),
        feature_group_count=channels,
        precision=lax.Precision.HIGHEST,
    )
    return result[0]


def gather_by_exchange(block, axis):
    count = lax.axis_size(axis)
    copies = jnp.broadcast_to(block[None], (count,) + block.shape)
    return lax.all_to_all(copies, axis, 0, 0, tiled=False)


def bf16_pieces(values, pieces):
    parts = []
    rest = values
    for _ in range(pieces):
        part = rest.astype(jnp.bfloat16)
        parts.append(part)
        rest = rest - part.astype(jnp.float32)
    return parts


def gather_by_shifts(block, axis):
    count = lax.axis_size(axis)
    position = lax.axis_index(axis)
    pieces = [block]
    for shift in range(1, count):
        pieces.append(
            lax.ppermute(block, axis, [(i, (i - shift) % count) for i in range(count)])
        )
    return jnp.roll(jnp.stack(pieces, 0), position, axis=0)


def reduce_by_shifts(blocks, rider, axis):
    count = lax.axis_size(axis)
    position = lax.axis_index(axis)
    total = lax.dynamic_index_in_dim(blocks, position, 0, keepdims=False).astype(jnp.float32)
    riders = rider.astype(jnp.float32)
    rows = blocks.shape[1]
    for shift in range(1, count):
        outgoing = lax.dynamic_index_in_dim(blocks, (position + shift) % count, 0, keepdims=False)
        outgoing = jnp.concatenate([outgoing, rider], 0)
        arrived = lax.ppermute(outgoing, axis, [(i, (i + shift) % count) for i in range(count)])
        total = total + arrived[:rows].astype(jnp.float32)
        riders = riders + arrived[rows:].astype(jnp.float32)
    return total, riders


def shifted_sum(padded, taps, span):
    total = taps[0][:, None] * padded[:, 0:span]
    for k in range(1, taps.shape[0]):
        total = total + taps[k][:, None] * padded[:, k : k + span]
    return total


def shards(signal, input_norm_gain, value_weight, gate_weight, depth_taps, cotangent):
    local_cols, frames = signal.shape
    groups = lax.axis_size("ch")
    blocks = lax.axis_size("seq")
    channel_position = lax.axis_index("ch")
    reach = depth_taps.shape[0] // 2
    gain_rows = jnp.stack(bf16_pieces(input_norm_gain, 3), 0)
    gain_rows = jnp.pad(gain_rows, ((0, 5), (0, frames - local_cols)))
    arrived = lax.all_gather(jnp.concatenate([signal, gain_rows], 0), "ch", axis=0)
    complete_signal = arrived[:, :local_cols].reshape(groups * local_cols, frames)
    gain_parts = arrived[:, local_cols : local_cols + 3, :local_cols].astype(jnp.float32)
    complete_gain = ((gain_parts[:, 0] + gain_parts[:, 1]) + gain_parts[:, 2]).reshape(-1)
    centered_unit, inverse_deviation = standardize_rows(complete_signal)
    normalized_signal = (centered_unit * complete_gain[:, None]).astype(jnp.bfloat16)
    centered_unit_rows = lax.dynamic_slice_in_dim(
        centered_unit, channel_position * local_cols, local_cols, 0
    )
    stacked = jnp.concatenate([value_weight, gate_weight], 1)
    gathered = gather_by_exchange(stacked, "seq").reshape(-1, stacked.shape[1])
    mixed = lax.dot_general(
        gathered, normalized_signal, (((0,), (0,)), ((), ())), preferred_element_type=jnp.float32
    )
    value = mixed[:local_cols]
    gate = mixed[local_cols:]
    sig_gate = jax.nn.sigmoid(gate)
    glued = (value * sig_gate).astype(jnp.bfloat16)
    glued_pad = extended(glued, (("seq", 1),), reach).astype(jnp.float32)
    span = glued.shape[1]
    taps_count = depth_taps.shape[0]
    pre = shifted_sum(glued_pad, depth_taps, span)
    sig_pre = jax.nn.sigmoid(pre)
    output = (pre * sig_pre).astype(jnp.bfloat16)
    grad_pre = (cotangent.astype(jnp.float32) * sig_pre * (1.0 + pre * (1.0 - sig_pre))).astype(
        jnp.bfloat16
    )
    grad_pre_f = grad_pre.astype(jnp.float32)
    grad_pad = extended(grad_pre, (("seq", 1),), reach).astype(jnp.float32)
    grad_glued = shifted_sum(grad_pad, depth_taps[::-1], span)
    tap_partial = jnp.stack(
        [jnp.sum(glued_pad[:, k : k + span] * grad_pre_f, 1) for k in range(taps_count)], 0
    )
    grad_v = (grad_glued * sig_gate).astype(jnp.bfloat16)
    grad_g = (grad_glued * value * sig_gate * (1.0 - sig_gate)).astype(jnp.bfloat16)
    grad_both = jnp.concatenate([grad_v, grad_g], 0)
    weight_partial = lax.dot_general(
        normalized_signal,
        grad_both,
        (((1,), (1,)), ((), ())),
        preferred_element_type=jnp.float32,
    )
    normed_term = jnp.dot(gathered, grad_both, preferred_element_type=jnp.float32).astype(
        jnp.bfloat16
    )
    width = weight_partial.shape[1]
    rows = value_weight.shape[0]
    taps_rows = depth_taps.shape[0]
    taps_flat = jnp.pad(tap_partial, ((0, 1), (0, 0))).reshape(blocks, -1)
    piece = taps_flat.shape[1]
    taps_row = jnp.concatenate(bf16_pieces(taps_flat, 3), 1)
    taps_row = jnp.pad(taps_row, ((0, 0), (0, width - taps_row.shape[1])))
    outgoing = jnp.concatenate(
        [weight_partial.astype(jnp.bfloat16).reshape(blocks, rows, width), taps_row[:, None]], 1
    )
    summed = jnp.sum(lax.all_to_all(outgoing, "seq", 0, 0, tiled=False).astype(jnp.float32), 0)
    weight_sums = summed[:rows]
    taps_summed = (summed[rows, :piece] + summed[rows, piece : 2 * piece]) + summed[
        rows, 2 * piece : 3 * piece
    ]
    grad_value = weight_sums[:, :local_cols]
    grad_gate = weight_sums[:, local_cols:]
    normed_f = normed_term.astype(jnp.float32)
    weighted = normed_f * complete_gain[:, None]
    own_moments = jnp.stack([jnp.sum(weighted, 0), jnp.sum(weighted * centered_unit, 0)], 0)
    moment_rows = jnp.concatenate(bf16_pieces(own_moments, 3), 0)
    half = frames // 2
    split = frames - frames // 4
    moment_rows = moment_rows.reshape(-1, frames - split)
    used_rows = moment_rows.shape[0]
    moment_rows = jnp.pad(moment_rows, ((0, 32 - used_rows), (0, 0)))
    early_part = lax.psum_scatter(
        normed_term[:, :split], "ch", scatter_dimension=0, tiled=True
    ).astype(jnp.float32)
    late_part, moment_total = reduce_by_shifts(
        normed_term[:, split:].reshape(groups, local_cols, frames - split), moment_rows, "ch"
    )
    normalized_gradient = jnp.concatenate([early_part, late_part], 1)
    moment_total = moment_total[:used_rows].reshape(6, frames)
    scaled_signal = normalized_gradient * input_norm_gain[:, None]
    moments = ((moment_total[0:2] + moment_total[2:4]) + moment_total[4:6]) * (
        1.0 / complete_signal.shape[0]
    )
    signal_gradient = (
        inverse_deviation
        * (scaled_signal - moments[0:1] - centered_unit_rows * moments[1:2])
    ).astype(jnp.bfloat16)
    gain_portion = jnp.sum(normalized_gradient * centered_unit_rows, 1)
    last = jnp.concatenate([taps_summed, gain_portion], 0)
    finished = gather_by_exchange(last, "seq")
    grad_taps = finished[:, :piece].reshape(-1)[: taps_rows * local_cols].reshape(
        taps_rows, local_cols
    )
    gain_gradient = jnp.sum(finished[:, piece:], 0)
    return (output, signal_gradient, grad_value, grad_gate, grad_taps, gain_gradient)


def solution(mesh):
    placed = (
        P("ch", "seq"),
        P("ch"),
        P("seq", "ch"),
        P("seq", "ch"),
        P(None, "ch"),
        P("ch", "seq"),
    )
    return jax.shard_map(
        shards,
        mesh=mesh,
        in_specs=placed,
        out_specs=(
            P("ch", "seq"),
            P("ch", "seq"),
            P("seq", "ch"),
            P("seq", "ch"),
            P(None, "ch"),
            P("ch"),
        ),
        check_vma=False,
    )
```
